128 devices in a mesh: cell: 32 (over z, y, core), gene: 4 (over x).
Axes of the slice: x: 4, y: 4, z: 4, core: 2. Of those that a mesh axis runs over, the one named last changes fastest.
Arguments:
- expression: bfloat16 [262144, 512], P('cell', 'gene'), may hold values from 0 to 9, as said below
- affinity: bfloat16 [4096, 256, 256], P('cell', 'gene'), may hold values from 0 to 1, as said below
- tile_rows: int32 [4096], P('cell'), may hold values from 0 to 1023, as said below
- tile_cols: int32 [4096], P('cell'), may hold values from 0 to 1023, as said below
- tile_count: int32 [32], P('cell'), may hold values from 35 to 125, as said below
Outputs:
- imputed: float32 [262144, 512], P('cell', 'gene')
The draws below stay inside these ranges and needn't reach their ends.
Inputs may be any that keep to these rules, and one draw needn't show every extreme that they name: `tile_rows`: the slots of index d of cell hold row blocks d * 32 to (d + 1) * 32 - 1. Among its first tile_count[d] slots each of those row blocks appears exactly once with itself as column block, and every other such slot names a column block of another index of cell. `tile_cols`: among the slots in use of one index of cell at most 3 name column blocks of any one other index, and on every index exactly 3 name those of some other index. A pair of blocks may repeat. `tile_count`: both ends are reached in every draw. `expression`: Positive. `affinity`: Positive.
All inputs are finite; a program needn't handle non-finite values.
Results may differ from the reference program's by a relative error of at most 0.0027.
Values may be sent and summed in bfloat16 or wider, within the bound.
No kernel may reach another device: no remote copies, remote signals or barrier semaphores. Data moves between devices by JAX's collectives and lax.ppermute only.
A program may use at most 192 MiB of HBM per device.

```python
import math
import jax
import jax.numpy as jnp
from jax import lax

G = 512
BS = 256
BLK_DEV = 32
REQ_CAP = 3
STEPS = 3
TILE_DEV = 128
BLOCKS = 1024
CELLS = 262144
TILES = 4096
N_CELL = 32


def tile_plan(key):
    base = jax.random.fold_in(key, 101)
    keys = jax.random.split(base, 7)
    device = jnp.arange(N_CELL, dtype=jnp.int32)
    full_dev = jax.random.randint(keys[6], (), 0, N_CELL)
    lean_dev = (full_dev + 1) % N_CELL
    upper = jax.random.randint(keys[0], (N_CELL, 1), 2, REQ_CAP + 1)
    per_peer = jnp.minimum(jax.random.randint(keys[1], (N_CELL, N_CELL), 0, REQ_CAP + 1), upper)
    per_peer = jnp.where((device == full_dev)[:, None], REQ_CAP, per_peer)
    per_peer = jnp.where((device == lean_dev)[:, None], 0, per_peer)
    forced = (device + 1 + jax.random.randint(keys[2], (N_CELL,), 0, N_CELL - 1)) % N_CELL
    per_peer = jnp.where(device[None, :] == forced[:, None], REQ_CAP, per_peer)
    per_peer = jnp.where(device[None, :] == device[:, None], 0, per_peer)
    place = jnp.arange(REQ_CAP, dtype=jnp.int32)
    live = (place[None, None, :] < per_peer[:, :, None]).reshape(N_CELL, N_CELL * REQ_CAP)
    peer = jnp.broadcast_to(device[None, :, None], (N_CELL, N_CELL, REQ_CAP)).reshape(N_CELL, N_CELL * REQ_CAP)
    col_slot = jax.random.randint(keys[3], (N_CELL, N_CELL * REQ_CAP), 0, BLK_DEV)
    row_slot = jax.random.randint(keys[4], (N_CELL, N_CELL * REQ_CAP), 0, BLK_DEV)
    far_cols = peer * BLK_DEV + col_slot
    far_rows = device[:, None] * BLK_DEV + row_slot
    own = device[:, None] * BLK_DEV + jnp.arange(BLK_DEV, dtype=jnp.int32)[None, :]
    cols = jnp.concatenate([own, far_cols], axis=1)
    rows = jnp.concatenate([own, far_rows], axis=1)
    valid = jnp.concatenate([jnp.ones((N_CELL, BLK_DEV), dtype=bool), live], axis=1)
    width = BLK_DEV + N_CELL * REQ_CAP
    index = jnp.arange(width, dtype=jnp.int32)[None, :]
    score = jax.random.randint(keys[5], (N_CELL, width), 0, width) * width + index
    score = jnp.where(valid, score, width * width + index)
    order = jnp.argsort(score, axis=1, stable=True)
    rows = jnp.take_along_axis(rows, order, axis=1)
    cols = jnp.take_along_axis(cols, order, axis=1)
    count = jnp.sum(valid.astype(jnp.int32), axis=1)
    return (rows.reshape(-1).astype(jnp.int32), cols.reshape(-1).astype(jnp.int32), count.astype(jnp.int32))


def draw_tile_rows(key, part):
    return tile_plan(key)[0]


def draw_tile_cols(key, part):
    return tile_plan(key)[1]


def draw_tile_count(key, part):
    return tile_plan(key)[2]


def draw_affinity(key, part):
    uniform_part = jax.random.uniform(jax.random.fold_in(key, 13), (TILES, BS, BS), jnp.float32, 0.0, 1.0)
    values = 0.001 + 0.999 * uniform_part ** 200.0
    return values.astype(jnp.bfloat16)


def draw_expression(key, part):
    first, second = jax.random.split(jax.random.fold_in(key, 7))
    block_scale = jnp.exp(jax.random.uniform(first, (BLOCKS, 1, G), jnp.float32, math.log(0.3), math.log(3.0)))
    noise = jnp.exp(jax.random.uniform(second, (BLOCKS, BS, G), jnp.float32, math.log(0.01), 0.0))
    rise = 1.0 + 2.0 * jnp.arange(BLOCKS, dtype=jnp.float32) / BLOCKS
    values = block_scale * noise * rise[:, None, None]
    return values.reshape(BLOCKS * BS, G).astype(jnp.bfloat16)


def setup_inputs(seed: int = 0) -> dict:
    arg_keys = jax.random.split(jax.random.key(seed), 6)
    expression = draw_expression(jax.random.fold_in(arg_keys[5], 71), 0)
    affinity = draw_affinity(jax.random.fold_in(arg_keys[5], 71), 0)
    tile_rows = draw_tile_rows(jax.random.fold_in(arg_keys[5], 71), 0)
    tile_cols = draw_tile_cols(jax.random.fold_in(arg_keys[5], 71), 0)
    tile_count = draw_tile_count(jax.random.fold_in(arg_keys[5], 71), 0)
    return {"expression": expression, "affinity": affinity, "tile_rows": tile_rows, "tile_cols": tile_cols, "tile_count": tile_count}


def reference(expression, affinity, tile_rows, tile_cols, tile_count):
    tiles = affinity.reshape(N_CELL, TILE_DEV, BS, BS)
    rows = tile_rows.reshape(N_CELL, TILE_DEV)
    cols = tile_cols.reshape(N_CELL, TILE_DEV)
    owners = jnp.arange(N_CELL, dtype=jnp.int32)
    eye = jnp.eye(BS, dtype=bool)

    def prepare(device_tiles, device_rows, device_cols, count):
        valid = jnp.arange(TILE_DEV, dtype=jnp.int32) < count
        selfish = (device_rows == device_cols)[:, None, None] & eye[None]
        keep = valid[:, None, None] & jnp.logical_not(selfish)
        return jnp.where(keep, device_tiles, jnp.zeros_like(device_tiles))

    def one_step(current, final):
        def per_device(item):
            device_tiles, device_rows, device_cols, count, owner = item
            masked = prepare(device_tiles, device_rows, device_cols, count)
            local_row = (device_rows - owner * BLK_DEV).astype(jnp.int32)
            sums = jnp.sum(masked.astype(jnp.float32), axis=-1)
            degree = jax.ops.segment_sum(sums, local_row, BLK_DEV)
            operand = current[device_cols].astype(jnp.float32)
            product = jnp.einsum("tij,tjg->tig", masked.astype(jnp.float32), operand)
            total = jax.ops.segment_sum(product, local_row, BLK_DEV)
            return total / degree[:, :, None]

        out = lax.map(per_device, (tiles, rows, cols, tile_count, owners))
        out = out.reshape(BLOCKS, BS, G)
        if final:
            return out
        return out.astype(jnp.bfloat16)

    current = expression.reshape(BLOCKS, BS, G)
    for step in range(STEPS):
        current = one_step(current, step == STEPS - 1)
    last = current.reshape(CELLS, G)
    top_start = jnp.max(expression.astype(jnp.float32), axis=0)
    top_end = jnp.max(last, axis=0)
    return last * (top_start / top_end)[None, :]
```

```python
import functools

import jax
import jax.numpy as jnp
from jax import lax
from jax.experimental import pallas as pl
from jax.experimental.pallas import tpu as pltpu
from jax.sharding import PartitionSpec as P

BS = 256
BLK_DEV = 32
REQ_CAP = 3
STEPS = 3
T_BLK = 16


def ranks_of(owner, remote):
    count = owner.shape[-1]
    order = jnp.arange(count, dtype=jnp.int32)
    earlier = order[None, :] < order[:, None]
    same = (owner[..., :, None] == owner[..., None, :]) & remote[..., None, :] & earlier
    return jnp.sum(same.astype(jnp.int32), axis=-1)


def step_kernel(first, src_ref, row_ref, kind_ref, a_ref, cur_ref, inc_ref, *rest):
    if first:
        out_ref, deg_ref, acc_ref = rest
    else:
        deg_ref, out_ref, acc_ref = rest
    s = pl.program_id(0)
    last = pl.num_programs(0) - 1

    @pl.when(s == 0)
    def _():
        acc_ref[...] = jnp.zeros_like(acc_ref)
        if first:
            deg_ref[...] = jnp.zeros_like(deg_ref)

    eye = lax.broadcasted_iota(jnp.int32, (BS, BS), 0) == lax.broadcasted_iota(jnp.int32, (BS, BS), 1)
    ones = jnp.ones((BS, acc_ref.shape[-1]), jnp.bfloat16)

    def contrib(r, a, x):
        acc_ref[r] += jnp.dot(a, x, preferred_element_type=jnp.float32)
        if first:
            deg_ref[r] += jnp.dot(a, ones, preferred_element_type=jnp.float32)

    def body(j, carry):
        t = s * T_BLK + j
        k = kind_ref[t]
        r = row_ref[t]
        c = src_ref[t]

        @pl.when(k == 1)
        def _():
            contrib(r, a_ref[j], cur_ref[c])

        @pl.when(k == 2)
        def _():
            a = a_ref[j]
            contrib(r, jnp.where(eye, jnp.zeros_like(a), a), cur_ref[c])

        @pl.when(k == 3)
        def _():
            contrib(r, a_ref[j], inc_ref[c])

        return carry

    lax.fori_loop(0, T_BLK, body, 0)

    @pl.when(s == last)
    def _():
        def fin(r, carry):
            out_ref[r] = (acc_ref[r] / deg_ref[r]).astype(out_ref.dtype)
            return carry

        lax.fori_loop(0, BLK_DEV, fin, 0)


def diffuse(tiles, current, incoming, deg, src, rows, kind, out_dtype):
    slots = tiles.shape[0]
    genes = current.shape[-1]
    first = deg is None
    full = lambda n: pl.BlockSpec((n, BS, genes), lambda s, *_: (0, 0, 0))
    in_specs = [
        pl.BlockSpec((T_BLK, BS, BS), lambda s, *_: (s, 0, 0)),
        full(current.shape[0]),
        full(incoming.shape[0]),
    ]
    args = [tiles, current, incoming]
    if first:
        out_specs = [full(BLK_DEV), full(BLK_DEV)]
        out_shape = [
            jax.ShapeDtypeStruct((BLK_DEV, BS, genes), out_dtype),
            jax.ShapeDtypeStruct((BLK_DEV, BS, genes), jnp.float32),
        ]
    else:
        in_specs.append(full(BLK_DEV))
        args.append(deg)
        out_specs = full(BLK_DEV)
        out_shape = jax.ShapeDtypeStruct((BLK_DEV, BS, genes), out_dtype)
    grid_spec = pltpu.PrefetchScalarGridSpec(
        num_scalar_prefetch=3,
        grid=(slots // T_BLK,),
        in_specs=in_specs,
        out_specs=out_specs,
        scratch_shapes=[pltpu.VMEM((BLK_DEV, BS, genes), jnp.float32)],
    )
    return pl.pallas_call(
        functools.partial(step_kernel, first),
        grid_spec=grid_spec,
        out_shape=out_shape,
        compiler_params=pltpu.CompilerParams(
            dimension_semantics=("arbitrary",), vmem_limit_bytes=56 * 1024 * 1024
        ),
    )(src, rows, kind, *args)


def on_device(expression, affinity, tile_rows, tile_cols, tile_count):
    me = lax.axis_index("cell")
    peers = lax.axis_size("cell")
    genes = expression.shape[1]
    tiles = lax.all_gather(affinity, "gene", axis=1, tiled=True)
    slots = tiles.shape[0]
    order = jnp.arange(slots, dtype=jnp.int32)
    valid = order < tile_count[0]
    local_row = tile_rows - me * BLK_DEV
    row_index = jnp.clip(jnp.where(valid, local_row, 0), 0, BLK_DEV - 1)
    owner = tile_cols // BLK_DEV
    col_slot = tile_cols - owner * BLK_DEV
    remote = valid & (owner != me)
    rank = ranks_of(owner, remote)
    peer_ids = jnp.arange(peers, dtype=jnp.int32)
    place = jnp.arange(REQ_CAP, dtype=jnp.int32)
    hit = (
        remote[:, None, None]
        & (owner[:, None, None] == peer_ids[None, :, None])
        & (rank[:, None, None] == place[None, None, :])
    )
    wanted = jnp.sum(jnp.where(hit, col_slot[:, None, None] + 1, 0), axis=0) - 1
    asked = lax.all_to_all(wanted, "cell", split_axis=0, concat_axis=0, tiled=True)
    asked = jnp.clip(asked, 0, BLK_DEV - 1)
    selfish = valid & (tile_rows == tile_cols)
    kind = jnp.where(remote, 3, jnp.where(selfish, 2, jnp.where(valid, 1, 0))).astype(jnp.int32)
    src = jnp.where(remote, owner * REQ_CAP + rank, jnp.where(valid, col_slot, 0))
    src = jnp.clip(src, 0, peers * REQ_CAP - 1)
    src = jnp.where(remote, src, jnp.clip(src, 0, BLK_DEV - 1)).astype(jnp.int32)
    current = expression.reshape(BLK_DEV, BS, genes)
    deg = None
    for step in range(STEPS):
        outgoing = current[asked]
        incoming = lax.all_to_all(outgoing, "cell", split_axis=0, concat_axis=0, tiled=True)
        incoming = incoming.reshape(peers * REQ_CAP, BS, genes)
        out_dtype = jnp.float32 if step == STEPS - 1 else jnp.bfloat16
        res = diffuse(tiles, current, incoming, deg, src, row_index, kind, out_dtype)
        if deg is None:
            current, deg = res
        else:
            current = res
    last = current.reshape(BLK_DEV * BS, genes)
    top_start = jnp.max(expression.astype(jnp.float32), axis=0)
    top_end = jnp.max(last, axis=0)
    top_start, top_end = lax.pmax((top_start, top_end), "cell")
    return last * (top_start / top_end)[None, :]


def solution(mesh):
    return jax.shard_map(
        on_device,
        mesh=mesh,
        in_specs=(P("cell", "gene"), P("cell", "gene", None), P("cell"), P("cell"), P("cell")),
        out_specs=P("cell", "gene"),
        check_vma=False,
    )
```

```python
import functools

import jax
import jax.numpy as jnp
from jax import lax
from jax.experimental import pallas as pl
from jax.experimental.pallas import tpu as pltpu
from jax.sharding import PartitionSpec as P

BS = 256
BLK_DEV = 32
REQ_CAP = 3
STEPS = 3
T_BLK = 16


def ranks_of(owner, remote):
    count = owner.shape[-1]
    order = jnp.arange(count, dtype=jnp.int32)
    earlier = order[None, :] < order[:, None]
    same = (owner[..., :, None] == owner[..., None, :]) & remote[..., None, :] & earlier
    return jnp.sum(same.astype(jnp.int32), axis=-1)


def step_kernel(final, src_ref, row_ref, kind_ref, ask_ref, a_ref, cur_ref, inc_ref, deg_ref, out_ref, side_ref, acc_ref):
    s = pl.program_id(0)
    last = pl.num_programs(0) - 1

    @pl.when(s == 0)
    def _():
        acc_ref[...] = jnp.zeros_like(acc_ref)

    eye = lax.broadcasted_iota(jnp.int32, (BS, BS), 0) == lax.broadcasted_iota(jnp.int32, (BS, BS), 1)

    def body(j, carry):
        t = s * T_BLK + j
        k = kind_ref[t]
        r = row_ref[t]
        c = src_ref[t]

        @pl.when(k == 1)
        def _():
            acc_ref[r] += jnp.dot(a_ref[j], cur_ref[c], preferred_element_type=jnp.float32)

        @pl.when(k == 2)
        def _():
            a = a_ref[j]
            a = jnp.where(eye, jnp.zeros_like(a), a)
            acc_ref[r] += jnp.dot(a, cur_ref[c], preferred_element_type=jnp.float32)

        @pl.when(k == 3)
        def _():
            acc_ref[r] += jnp.dot(a_ref[j], inc_ref[c], preferred_element_type=jnp.float32)

        return carry

    lax.fori_loop(0, T_BLK, body, 0)

    @pl.when(s == last)
    def _():
        if final:
            def fin(r, m):
                val = acc_ref[r] / deg_ref[r]
                out_ref[r] = val
                return jnp.maximum(m, jnp.max(val, axis=0, keepdims=True))

            m = lax.fori_loop(0, BLK_DEV, fin, jnp.full((1, out_ref.shape[-1]), -jnp.inf, jnp.float32))
            side_ref[...] = jnp.broadcast_to(m, side_ref.shape)
        else:
            def fin(r, carry):
                out_ref[r] = (acc_ref[r] / deg_ref[r]).astype(out_ref.dtype)
                return carry

            lax.fori_loop(0, BLK_DEV, fin, 0)

            def send(q, carry):
                side_ref[q] = out_ref[ask_ref[q]]
                return carry

            lax.fori_loop(0, side_ref.shape[0], send, 0)


def diffuse(tiles, current, incoming, deg, src, rows, kind, asked, final):
    slots = tiles.shape[0]
    genes = current.shape[-1]
    n_ask = incoming.shape[0]

    def full(n):
        return pl.BlockSpec((n, BS, genes), lambda s, *_: (0, 0, 0), pipeline_mode=pl.Buffered(1))

    in_specs = [
        pl.BlockSpec((T_BLK, BS, BS), lambda s, *_: (s, 0, 0)),
        full(current.shape[0]),
        full(n_ask),
        full(BLK_DEV),
    ]
    out_block = pl.BlockSpec((BLK_DEV, BS, genes), lambda s, *_: (0, 0, 0))
    if final:
        out_specs = [out_block, pl.BlockSpec((8, genes), lambda s, *_: (0, 0))]
        out_shape = [
            jax.ShapeDtypeStruct((BLK_DEV, BS, genes), jnp.float32),
            jax.ShapeDtypeStruct((8, genes), jnp.float32),
        ]
    else:
        out_specs = [out_block, pl.BlockSpec((n_ask, BS, genes), lambda s, *_: (0, 0, 0))]
        out_shape = [
            jax.ShapeDtypeStruct((BLK_DEV, BS, genes), jnp.bfloat16),
            jax.ShapeDtypeStruct((n_ask, BS, genes), jnp.bfloat16),
        ]
    grid_spec = pltpu.PrefetchScalarGridSpec(
        num_scalar_prefetch=4,
        grid=(slots // T_BLK,),
        in_specs=in_specs,
        out_specs=out_specs,
        scratch_shapes=[pltpu.VMEM((BLK_DEV, BS, genes), jnp.float32)],
    )
    return pl.pallas_call(
        functools.partial(step_kernel, final),
        grid_spec=grid_spec,
        out_shape=out_shape,
        compiler_params=pltpu.CompilerParams(
            dimension_semantics=("arbitrary",), vmem_limit_bytes=60 * 1024 * 1024
        ),
    )(src, rows, kind, asked, tiles, current, incoming, deg)


def on_device(expression, affinity, tile_rows, tile_cols, tile_count):
    me = lax.axis_index("cell")
    gi = lax.axis_index("gene")
    peers = lax.axis_size("cell")
    genes = expression.shape[1]
    part_rows = affinity.shape[1]
    tiles = lax.all_gather(affinity, "gene", axis=1, tiled=True)
    slots = tiles.shape[0]
    order = jnp.arange(slots, dtype=jnp.int32)
    valid = order < tile_count[0]
    local_row = tile_rows - me * BLK_DEV
    row_index = jnp.clip(jnp.where(valid, local_row, 0), 0, BLK_DEV - 1)
    owner = tile_cols // BLK_DEV
    col_slot = tile_cols - owner * BLK_DEV
    remote = valid & (owner != me)
    selfish = valid & (tile_rows == tile_cols)

    diag = (
        lax.broadcasted_iota(jnp.int32, (part_rows, BS), 0) + gi * part_rows
        == lax.broadcasted_iota(jnp.int32, (part_rows, BS), 1)
    )
    keep = valid[:, None, None] & jnp.logical_not(selfish[:, None, None] & diag[None])
    part_sums = jnp.sum(jnp.where(keep, affinity, jnp.zeros_like(affinity)), axis=-1, dtype=jnp.float32)
    part_deg = jax.ops.segment_sum(part_sums, row_index, BLK_DEV)
    deg = lax.all_gather(part_deg, "gene", axis=1, tiled=True)
    deg = jnp.broadcast_to(deg[:, :, None], (BLK_DEV, BS, genes))

    rank = ranks_of(owner, remote)
    peer_ids = jnp.arange(peers, dtype=jnp.int32)
    place = jnp.arange(REQ_CAP, dtype=jnp.int32)
    hit = (
        remote[:, None, None]
        & (owner[:, None, None] == peer_ids[None, :, None])
        & (rank[:, None, None] == place[None, None, :])
    )
    wanted = jnp.sum(jnp.where(hit, col_slot[:, None, None] + 1, 0), axis=0) - 1
    top_start = jnp.max(expression, axis=0).astype(jnp.float32)
    request = jnp.concatenate(
        [wanted.astype(jnp.float32), jnp.broadcast_to(top_start[None, :], (peers, genes))], axis=1
    )
    reply = lax.all_to_all(request, "cell", split_axis=0, concat_axis=0, tiled=True)
    asked = jnp.clip(reply[:, :REQ_CAP].astype(jnp.int32), 0, BLK_DEV - 1).reshape(-1)
    top_start = jnp.max(reply[:, REQ_CAP:], axis=0)

    kind = jnp.where(remote, 3, jnp.where(selfish, 2, jnp.where(valid, 1, 0))).astype(jnp.int32)
    src = jnp.where(remote, owner * REQ_CAP + rank, jnp.where(valid, col_slot, 0))
    src = jnp.where(remote, jnp.clip(src, 0, peers * REQ_CAP - 1), jnp.clip(src, 0, BLK_DEV - 1)).astype(jnp.int32)

    current = expression.reshape(BLK_DEV, BS, genes)
    outgoing = current[asked]
    for step in range(STEPS):
        incoming = lax.all_to_all(
            outgoing.reshape(peers, REQ_CAP, BS, genes), "cell", split_axis=0, concat_axis=0, tiled=True
        )
        incoming = incoming.reshape(peers * REQ_CAP, BS, genes)
        final = step == STEPS - 1
        current, side = diffuse(tiles, current, incoming, deg, src, row_index, kind, asked, final)
        outgoing = side
    last = current.reshape(BLK_DEV * BS, genes)
    top_end = side[0]
    top_end = jnp.max(
        lax.all_to_all(jnp.broadcast_to(top_end[None, :], (peers, genes)), "cell", 0, 0, tiled=True), axis=0
    )
    return last * (top_start / top_end)[None, :]


def solution(mesh):
    return jax.shard_map(
        on_device,
        mesh=mesh,
        in_specs=(P("cell", "gene"), P("cell", "gene", None), P("cell"), P("cell"), P("cell")),
        out_specs=P("cell", "gene"),
        check_vma=False,
    )
```

```python
import functools

import jax
import jax.numpy as jnp
from jax import lax
from jax.experimental import pallas as pl
from jax.experimental.pallas import tpu as pltpu
from jax.sharding import PartitionSpec as P

BS = 256
BLK_DEV = 32
REQ_CAP = 3
STEPS = 3
T_BLK = 16
UNROLL = 4


def ranks_of(owner, remote):
    count = owner.shape[-1]
    order = jnp.arange(count, dtype=jnp.int32)
    earlier = order[None, :] < order[:, None]
    same = (owner[..., :, None] == owner[..., None, :]) & remote[..., None, :] & earlier
    return jnp.sum(same.astype(jnp.int32), axis=-1)


def step_kernel(final, src_ref, row_ref, kind_ref, ask_ref, a_ref, cur_ref, inc_ref, deg_ref, out_ref, side_ref, acc_ref):
    s = pl.program_id(0)
    last = pl.num_programs(0) - 1

    @pl.when(s == 0)
    def _():
        acc_ref[...] = jnp.zeros_like(acc_ref)

    def body(j, carry):
        t = s * T_BLK + j
        r = row_ref[t]
        c = src_ref[t]
        x = jnp.where(kind_ref[t] == 3, inc_ref[c], cur_ref[jnp.minimum(c, BLK_DEV - 1)])
        acc_ref[r] += jnp.dot(a_ref[j], x, preferred_element_type=jnp.float32)
        return carry

    lax.fori_loop(0, T_BLK, body, 0, unroll=UNROLL)

    @pl.when(s == last)
    def _():
        if final:
            def fin(r, m):
                val = acc_ref[r] / deg_ref[r]
                out_ref[r] = val
                return jnp.maximum(m, jnp.max(val, axis=0, keepdims=True))

            m = lax.fori_loop(0, BLK_DEV, fin, jnp.full((1, out_ref.shape[-1]), -jnp.inf, jnp.float32))
            side_ref[...] = jnp.broadcast_to(m, side_ref.shape)
        else:
            def fin(r, carry):
                out_ref[r] = (acc_ref[r] / deg_ref[r]).astype(out_ref.dtype)
                return carry

            lax.fori_loop(0, BLK_DEV, fin, 0)

            def send(q, carry):
                side_ref[q] = out_ref[ask_ref[q]]
                return carry

            lax.fori_loop(0, side_ref.shape[0], send, 0)


def diffuse(tiles, current, incoming, deg, src, rows, kind, asked, final):
    slots = tiles.shape[0]
    genes = current.shape[-1]
    n_ask = incoming.shape[0]

    def full(n):
        return pl.BlockSpec((n, BS, genes), lambda s, *_: (0, 0, 0), pipeline_mode=pl.Buffered(1))

    in_specs = [
        pl.BlockSpec((T_BLK, BS, BS), lambda s, *_: (s, 0, 0)),
        full(current.shape[0]),
        full(n_ask),
        full(BLK_DEV),
    ]
    out_block = pl.BlockSpec((BLK_DEV, BS, genes), lambda s, *_: (0, 0, 0))
    if final:
        out_specs = [out_block, pl.BlockSpec((8, genes), lambda s, *_: (0, 0))]
        out_shape = [
            jax.ShapeDtypeStruct((BLK_DEV, BS, genes), jnp.float32),
            jax.ShapeDtypeStruct((8, genes), jnp.float32),
        ]
    else:
        out_specs = [out_block, pl.BlockSpec((n_ask, BS, genes), lambda s, *_: (0, 0, 0))]
        out_shape = [
            jax.ShapeDtypeStruct((BLK_DEV, BS, genes), jnp.bfloat16),
            jax.ShapeDtypeStruct((n_ask, BS, genes), jnp.bfloat16),
        ]
    grid_spec = pltpu.PrefetchScalarGridSpec(
        num_scalar_prefetch=4,
        grid=(slots // T_BLK,),
        in_specs=in_specs,
        out_specs=out_specs,
        scratch_shapes=[pltpu.VMEM((BLK_DEV, BS, genes), jnp.float32)],
    )
    return pl.pallas_call(
        functools.partial(step_kernel, final),
        grid_spec=grid_spec,
        out_shape=out_shape,
        compiler_params=pltpu.CompilerParams(
            dimension_semantics=("arbitrary",), vmem_limit_bytes=60 * 1024 * 1024
        ),
    )(src, rows, kind, asked, tiles, current, incoming, deg)


def on_device(expression, affinity, tile_rows, tile_cols, tile_count):
    me = lax.axis_index("cell")
    gi = lax.axis_index("gene")
    peers = lax.axis_size("cell")
    genes = expression.shape[1]
    part_rows = affinity.shape[1]
    slots = affinity.shape[0]
    order = jnp.arange(slots, dtype=jnp.int32)
    valid = order < tile_count[0]
    local_row = tile_rows - me * BLK_DEV
    row_index = jnp.clip(jnp.where(valid, local_row, 0), 0, BLK_DEV - 1)
    owner = tile_cols // BLK_DEV
    col_slot = tile_cols - owner * BLK_DEV
    remote = valid & (owner != me)
    selfish = valid & (tile_rows == tile_cols)

    diag = (
        lax.broadcasted_iota(jnp.int32, (part_rows, BS), 0) + gi * part_rows
        == lax.broadcasted_iota(jnp.int32, (part_rows, BS), 1)
    )
    keep = valid[:, None, None] & jnp.logical_not(selfish[:, None, None] & diag[None])
    masked = jnp.where(keep, affinity, jnp.zeros_like(affinity))
    tiles = lax.all_gather(masked, "gene", axis=1, tiled=True)
    part_sums = jnp.sum(masked, axis=-1, dtype=jnp.float32)
    part_deg = jax.ops.segment_sum(part_sums, row_index, BLK_DEV)
    deg = lax.all_gather(part_deg, "gene", axis=1, tiled=True)
    deg = jnp.broadcast_to(deg[:, :, None], (BLK_DEV, BS, genes))

    rank = ranks_of(owner, remote)
    peer_ids = jnp.arange(peers, dtype=jnp.int32)
    place = jnp.arange(REQ_CAP, dtype=jnp.int32)
    hit = (
        remote[:, None, None]
        & (owner[:, None, None] == peer_ids[None, :, None])
        & (rank[:, None, None] == place[None, None, :])
    )
    wanted = jnp.sum(jnp.where(hit, col_slot[:, None, None] + 1, 0), axis=0) - 1
    top_start = jnp.max(expression, axis=0).astype(jnp.float32)
    request = jnp.concatenate(
        [wanted.astype(jnp.float32), jnp.broadcast_to(top_start[None, :], (peers, genes))], axis=1
    )
    reply = lax.all_to_all(request, "cell", split_axis=0, concat_axis=0, tiled=True)
    asked = jnp.clip(reply[:, :REQ_CAP].astype(jnp.int32), 0, BLK_DEV - 1).reshape(-1)
    top_start = jnp.max(reply[:, REQ_CAP:], axis=0)

    kind = jnp.where(remote, 3, jnp.where(selfish, 2, jnp.where(valid, 1, 0))).astype(jnp.int32)
    src = jnp.where(remote, owner * REQ_CAP + rank, jnp.where(valid, col_slot, 0))
    src = jnp.where(remote, jnp.clip(src, 0, peers * REQ_CAP - 1), jnp.clip(src, 0, BLK_DEV - 1)).astype(jnp.int32)

    current = expression.reshape(BLK_DEV, BS, genes)
    outgoing = current[asked]
    for step in range(STEPS):
        incoming = lax.all_to_all(
            outgoing.reshape(peers, REQ_CAP, BS, genes), "cell", split_axis=0, concat_axis=0, tiled=True
        )
        incoming = incoming.reshape(peers * REQ_CAP, BS, genes)
        final = step == STEPS - 1
        current, side = diffuse(tiles, current, incoming, deg, src, row_index, kind, asked, final)
        outgoing = side
    last = current.reshape(BLK_DEV * BS, genes)
    top_end = side[0]
    top_end = jnp.max(
        lax.all_to_all(jnp.broadcast_to(top_end[None, :], (peers, genes)), "cell", 0, 0, tiled=True), axis=0
    )
    return last * (top_start / top_end)[None, :]


def solution(mesh):
    return jax.shard_map(
        on_device,
        mesh=mesh,
        in_specs=(P("cell", "gene"), P("cell", "gene", None), P("cell"), P("cell"), P("cell")),
        out_specs=P("cell", "gene"),
        check_vma=False,
    )
```

```python
import functools

import jax
import jax.numpy as jnp
from jax import lax
from jax.experimental import pallas as pl
from jax.experimental.pallas import tpu as pltpu
from jax.sharding import PartitionSpec as P

BS = 256
BLK_DEV = 32
REQ_CAP = 3
STEPS = 3
T_BLK = 16
UNROLL = 4


def ranks_of(owner, remote):
    count = owner.shape[-1]
    order = jnp.arange(count, dtype=jnp.int32)
    earlier = order[None, :] < order[:, None]
    same = (owner[..., :, None] == owner[..., None, :]) & remote[..., None, :] & earlier
    return jnp.sum(same.astype(jnp.int32), axis=-1)


def step_kernel(final, src_ref, row_ref, kind_ref, ask_ref, a_ref, cur_ref, inc_ref, deg_ref, out_ref, side_ref, acc_ref):
    s = pl.program_id(0)
    last = pl.num_programs(0) - 1

    @pl.when(s == 0)
    def _():
        acc_ref[...] = jnp.zeros_like(acc_ref)

    def body(j, carry):
        t = s * T_BLK + j
        r = row_ref[t]
        c = src_ref[t]
        x = jnp.where(kind_ref[t] == 3, inc_ref[c], cur_ref[jnp.minimum(c, BLK_DEV - 1)])
        acc_ref[r] += jnp.dot(a_ref[j], x, preferred_element_type=jnp.float32)
        return carry

    lax.fori_loop(0, T_BLK, body, 0, unroll=UNROLL)

    @pl.when(s == last)
    def _():
        if final:
            def fin(r, m):
                val = acc_ref[r] / deg_ref[r]
                out_ref[r] = val
                return jnp.maximum(m, jnp.max(val, axis=0, keepdims=True))

            m = lax.fori_loop(0, BLK_DEV, fin, jnp.full((1, out_ref.shape[-1]), -jnp.inf, jnp.float32))
            side_ref[...] = jnp.broadcast_to(m, side_ref.shape)
        else:
            def fin(r, carry):
                out_ref[r] = (acc_ref[r] / deg_ref[r]).astype(out_ref.dtype)
                return carry

            lax.fori_loop(0, BLK_DEV, fin, 0)

            def send(q, carry):
                side_ref[q] = out_ref[ask_ref[q]]
                return carry

            lax.fori_loop(0, side_ref.shape[0], send, 0)


def diffuse(tiles, current, incoming, deg, src, rows, kind, asked, final):
    slots = tiles.shape[0]
    genes = current.shape[-1]
    n_ask = incoming.shape[0]

    def full(n):
        return pl.BlockSpec((n, BS, genes), lambda s, *_: (0, 0, 0), pipeline_mode=pl.Buffered(1))

    in_specs = [
        pl.BlockSpec((T_BLK, BS, BS), lambda s, *_: (s, 0, 0)),
        full(current.shape[0]),
        full(n_ask),
        full(BLK_DEV),
    ]
    out_block = pl.BlockSpec((BLK_DEV, BS, genes), lambda s, *_: (0, 0, 0))
    if final:
        out_specs = [out_block, pl.BlockSpec((8, genes), lambda s, *_: (0, 0))]
        out_shape = [
            jax.ShapeDtypeStruct((BLK_DEV, BS, genes), jnp.float32),
            jax.ShapeDtypeStruct((8, genes), jnp.float32),
        ]
    else:
        out_specs = [out_block, pl.BlockSpec((n_ask, BS, genes), lambda s, *_: (0, 0, 0))]
        out_shape = [
            jax.ShapeDtypeStruct((BLK_DEV, BS, genes), jnp.bfloat16),
            jax.ShapeDtypeStruct((n_ask, BS, genes), jnp.bfloat16),
        ]
    grid_spec = pltpu.PrefetchScalarGridSpec(
        num_scalar_prefetch=4,
        grid=(slots // T_BLK,),
        in_specs=in_specs,
        out_specs=out_specs,
        scratch_shapes=[pltpu.VMEM((BLK_DEV, BS, genes), jnp.float32)],
    )
    return pl.pallas_call(
        functools.partial(step_kernel, final),
        grid_spec=grid_spec,
        out_shape=out_shape,
        compiler_params=pltpu.CompilerParams(
            dimension_semantics=("arbitrary",), vmem_limit_bytes=60 * 1024 * 1024
        ),
    )(src, rows, kind, asked, tiles, current, incoming, deg)


def on_device(expression, affinity, tile_rows, tile_cols, tile_count):
    me = lax.axis_index("cell")
    gi = lax.axis_index("gene")
    peers = lax.axis_size("cell")
    genes = expression.shape[1]
    part_rows = affinity.shape[1]
    slots = affinity.shape[0]
    order = jnp.arange(slots, dtype=jnp.int32)
    valid = order < tile_count[0]
    local_row = tile_rows - me * BLK_DEV
    row_index = jnp.clip(jnp.where(valid, local_row, 0), 0, BLK_DEV - 1)
    owner = tile_cols // BLK_DEV
    col_slot = tile_cols - owner * BLK_DEV
    remote = valid & (owner != me)
    selfish = valid & (tile_rows == tile_cols)

    diag = (
        lax.broadcasted_iota(jnp.int32, (part_rows, BS), 0) + gi * part_rows
        == lax.broadcasted_iota(jnp.int32, (part_rows, BS), 1)
    )
    keep = valid[:, None, None] & jnp.logical_not(selfish[:, None, None] & diag[None])
    masked = jnp.where(keep, affinity, jnp.zeros_like(affinity))
    tiles = lax.all_gather(masked, "gene", axis=1, tiled=True)
    part_sums = jnp.sum(masked, axis=-1, dtype=jnp.float32)
    part_deg = jax.ops.segment_sum(part_sums, row_index, BLK_DEV)
    deg = lax.all_gather(part_deg, "gene", axis=1, tiled=True)
    deg = jnp.broadcast_to(deg[:, :, None], (BLK_DEV, BS, genes))

    rank = ranks_of(owner, remote)
    peer_ids = jnp.arange(peers, dtype=jnp.int32)
    place = jnp.arange(REQ_CAP, dtype=jnp.int32)
    hit = (
        remote[:, None, None]
        & (owner[:, None, None] == peer_ids[None, :, None])
        & (rank[:, None, None] == place[None, None, :])
    )
    wanted = jnp.sum(jnp.where(hit, col_slot[:, None, None] + 1, 0), axis=0) - 1
    top_start = jnp.max(expression, axis=0).astype(jnp.float32)
    request = jnp.concatenate(
        [wanted.astype(jnp.float32), jnp.broadcast_to(top_start[None, :], (peers, genes))], axis=1
    )
    reply = lax.all_to_all(request, "cell", split_axis=0, concat_axis=0, tiled=True)
    asked = jnp.clip(reply[:, :REQ_CAP].astype(jnp.int32), 0, BLK_DEV - 1).reshape(-1)
    top_start = jnp.max(reply[:, REQ_CAP:], axis=0)

    kind = jnp.where(remote, 3, jnp.where(selfish, 2, jnp.where(valid, 1, 0))).astype(jnp.int32)
    src = jnp.where(remote, owner * REQ_CAP + rank, jnp.where(valid, col_slot, 0))
    src = jnp.where(remote, jnp.clip(src, 0, peers * REQ_CAP - 1), jnp.clip(src, 0, BLK_DEV - 1)).astype(jnp.int32)

    halves = 2
    width = genes // halves
    expr = expression.reshape(BLK_DEV, BS, genes)
    deg = deg[:, :, :width]
    currents = [expr[:, :, h * width:(h + 1) * width] for h in range(halves)]
    outgoings = [c[asked] for c in currents]
    sides = [None] * halves
    for step in range(STEPS):
        final = step == STEPS - 1
        for h in range(halves):
            incoming = lax.all_to_all(
                outgoings[h].reshape(peers, REQ_CAP, BS, width), "cell", split_axis=0, concat_axis=0, tiled=True
            )
            incoming = incoming.reshape(peers * REQ_CAP, BS, width)
            currents[h], sides[h] = diffuse(tiles, currents[h], incoming, deg, src, row_index, kind, asked, final)
            outgoings[h] = sides[h]
    last = jnp.concatenate(currents, axis=-1).reshape(BLK_DEV * BS, genes)
    top_end = jnp.concatenate([sd[0] for sd in sides], axis=-1)
    top_end = jnp.max(
        lax.all_to_all(jnp.broadcast_to(top_end[None, :], (peers, genes)), "cell", 0, 0, tiled=True), axis=0
    )
    return last * (top_start / top_end)[None, :]


def solution(mesh):
    return jax.shard_map(
        on_device,
        mesh=mesh,
        in_specs=(P("cell", "gene"), P("cell", "gene", None), P("cell"), P("cell"), P("cell")),
        out_specs=P("cell", "gene"),
        check_vma=False,
    )
```

```python
import functools

import jax
import jax.numpy as jnp
from jax import lax
from jax.experimental import pallas as pl
from jax.experimental.pallas import tpu as pltpu
from jax.sharding import PartitionSpec as P

BS = 256
BLK_DEV = 32
REQ_CAP = 3
STEPS = 3
UNROLL = 5


def ranks_of(owner, remote):
    count = owner.shape[-1]
    order = jnp.arange(count, dtype=jnp.int32)
    earlier = order[None, :] < order[:, None]
    same = (owner[..., :, None] == owner[..., None, :]) & remote[..., None, :] & earlier
    return jnp.sum(same.astype(jnp.int32), axis=-1)


def step_kernel(final, t_blk, src_ref, row_ref, kind_ref, ask_ref, a_ref, cur_ref, inc_ref, deg_ref, out_ref, side_ref, acc_ref):
    s = pl.program_id(0)
    last = pl.num_programs(0) - 1

    @pl.when(s == 0)
    def _():
        acc_ref[...] = jnp.zeros_like(acc_ref)

    def body(j, carry):
        t = s * t_blk + j
        r = row_ref[t]
        c = src_ref[t]
        x = jnp.where(kind_ref[t] == 3, inc_ref[c], cur_ref[jnp.minimum(c, BLK_DEV - 1)])
        acc_ref[r] += jnp.dot(a_ref[j], x, preferred_element_type=jnp.float32)
        return carry

    lax.fori_loop(0, t_blk, body, 0, unroll=UNROLL)

    @pl.when(s == last)
    def _():
        deg_cols = deg_ref[...].T
        m = jnp.full((1, out_ref.shape[-1]), -jnp.inf, jnp.float32)
        for r in range(BLK_DEV):
            val = acc_ref[r] / deg_cols[:, r:r + 1]
            out_ref[r] = val.astype(out_ref.dtype)
            if final:
                m = jnp.maximum(m, jnp.max(val, axis=0, keepdims=True))
        if final:
            side_ref[...] = jnp.broadcast_to(m, side_ref.shape)
        else:
            def send(q, carry):
                side_ref[q] = out_ref[ask_ref[q]]
                return carry

            lax.fori_loop(0, side_ref.shape[0], send, 0)


def diffuse(tiles, current, incoming, deg, src, rows, kind, asked, final, t_blk):
    slots = tiles.shape[0]
    genes = current.shape[-1]
    n_ask = incoming.shape[0]

    def full(n):
        return pl.BlockSpec((n, BS, genes), lambda s, *_: (0, 0, 0), pipeline_mode=pl.Buffered(1))

    in_specs = [
        pl.BlockSpec((t_blk, BS, BS), lambda s, *_: (s, 0, 0)),
        full(current.shape[0]),
        full(n_ask),
        pl.BlockSpec(deg.shape, lambda s, *_: (0, 0), pipeline_mode=pl.Buffered(1)),
    ]
    out_block = pl.BlockSpec((BLK_DEV, BS, genes), lambda s, *_: (0, 0, 0))
    if final:
        out_specs = [out_block, pl.BlockSpec((8, genes), lambda s, *_: (0, 0))]
        out_shape = [
            jax.ShapeDtypeStruct((BLK_DEV, BS, genes), jnp.float32),
            jax.ShapeDtypeStruct((8, genes), jnp.float32),
        ]
    else:
        out_specs = [out_block, pl.BlockSpec((n_ask, BS, genes), lambda s, *_: (0, 0, 0))]
        out_shape = [
            jax.ShapeDtypeStruct((BLK_DEV, BS, genes), jnp.bfloat16),
            jax.ShapeDtypeStruct((n_ask, BS, genes), jnp.bfloat16),
        ]
    grid_spec = pltpu.PrefetchScalarGridSpec(
        num_scalar_prefetch=4,
        grid=(slots // t_blk,),
        in_specs=in_specs,
        out_specs=out_specs,
        scratch_shapes=[pltpu.VMEM((BLK_DEV + 1, BS, genes), jnp.float32)],
    )
    return pl.pallas_call(
        functools.partial(step_kernel, final, t_blk),
        grid_spec=grid_spec,
        out_shape=out_shape,
        compiler_params=pltpu.CompilerParams(
            dimension_semantics=("arbitrary",), vmem_limit_bytes=60 * 1024 * 1024
        ),
    )(src, rows, kind, asked, tiles, current, incoming, deg)


def on_device(expression, affinity, tile_rows, tile_cols, tile_count):
    me = lax.axis_index("cell")
    gi = lax.axis_index("gene")
    peers = lax.axis_size("cell")
    genes = expression.shape[1]
    part_rows = affinity.shape[1]
    slots = affinity.shape[0]
    order = jnp.arange(slots, dtype=jnp.int32)
    valid = order < tile_count[0]
    local_row = tile_rows - me * BLK_DEV
    row_index = jnp.clip(jnp.where(valid, local_row, 0), 0, BLK_DEV - 1)
    junk_row = jnp.where(valid, row_index, BLK_DEV).astype(jnp.int32)
    used = min(slots, BLK_DEV + (peers - 1) * REQ_CAP)
    t_blk = max(d for d in range(1, 33) if used % d == 0)
    owner = tile_cols // BLK_DEV
    col_slot = tile_cols - owner * BLK_DEV
    remote = valid & (owner != me)
    selfish = valid & (tile_rows == tile_cols)

    diag = (
        lax.broadcasted_iota(jnp.int32, (part_rows, BS), 0) + gi * part_rows
        == lax.broadcasted_iota(jnp.int32, (part_rows, BS), 1)
    )
    keep = valid[:, None, None] & jnp.logical_not(selfish[:, None, None] & diag[None])
    masked = jnp.where(keep, affinity, jnp.zeros_like(affinity))
    tiles = lax.all_gather(masked[:used], "gene", axis=1, tiled=True)
    part_sums = jnp.sum(masked, axis=-1, dtype=jnp.float32)
    part_deg = jax.ops.segment_sum(part_sums, row_index, BLK_DEV)
    deg = lax.all_gather(part_deg, "gene", axis=1, tiled=True)

    rank = ranks_of(owner, remote)
    peer_ids = jnp.arange(peers, dtype=jnp.int32)
    place = jnp.arange(REQ_CAP, dtype=jnp.int32)
    hit = (
        remote[:, None, None]
        & (owner[:, None, None] == peer_ids[None, :, None])
        & (rank[:, None, None] == place[None, None, :])
    )
    wanted = jnp.sum(jnp.where(hit, col_slot[:, None, None] + 1, 0), axis=0) - 1
    top_start = jnp.max(expression, axis=0).astype(jnp.float32)
    request = jnp.concatenate(
        [wanted.astype(jnp.float32), jnp.broadcast_to(top_start[None, :], (peers, genes))], axis=1
    )
    reply = lax.all_to_all(request, "cell", split_axis=0, concat_axis=0, tiled=True)
    asked = jnp.clip(reply[:, :REQ_CAP].astype(jnp.int32), 0, BLK_DEV - 1).reshape(-1)
    top_start = jnp.max(reply[:, REQ_CAP:], axis=0)

    kind = jnp.where(remote, 3, jnp.where(selfish, 2, jnp.where(valid, 1, 0))).astype(jnp.int32)
    src = jnp.where(remote, owner * REQ_CAP + rank, jnp.where(valid, col_slot, 0))
    src = jnp.where(remote, jnp.clip(src, 0, peers * REQ_CAP - 1), jnp.clip(src, 0, BLK_DEV - 1)).astype(jnp.int32)

    current = expression.reshape(BLK_DEV, BS, genes)
    outgoing = current[asked]
    for step in range(STEPS):
        incoming = lax.all_to_all(
            outgoing.reshape(peers, REQ_CAP, BS, genes), "cell", split_axis=0, concat_axis=0, tiled=True
        )
        incoming = incoming.reshape(peers * REQ_CAP, BS, genes)
        final = step == STEPS - 1
        current, side = diffuse(tiles, current, incoming, deg, src, junk_row, kind, asked, final, t_blk)
        outgoing = side
    last = current.reshape(BLK_DEV * BS, genes)
    top_end = side[0]
    top_end = jnp.max(
        lax.all_to_all(jnp.broadcast_to(top_end[None, :], (peers, genes)), "cell", 0, 0, tiled=True), axis=0
    )
    return last * (top_start / top_end)[None, :]


def solution(mesh):
    return jax.shard_map(
        on_device,
        mesh=mesh,
        in_specs=(P("cell", "gene"), P("cell", "gene", None), P("cell"), P("cell"), P("cell")),
        out_specs=P("cell", "gene"),
        check_vma=False,
    )
```

```python
import functools

import jax
import jax.numpy as jnp
from jax import lax
from jax.experimental import pallas as pl
from jax.experimental.pallas import tpu as pltpu
from jax.sharding import PartitionSpec as P

BS = 256
BLK_DEV = 32
REQ_CAP = 3
STEPS = 3
UNROLL = 5
HALF = BS // 2
CHUNK = 32


def ranks_of(owner, remote):
    count = owner.shape[-1]
    order = jnp.arange(count, dtype=jnp.int32)
    earlier = order[None, :] < order[:, None]
    same = (owner[..., :, None] == owner[..., None, :]) & remote[..., None, :] & earlier
    return jnp.sum(same.astype(jnp.int32), axis=-1)


def interleave(first, second):
    pieces = []
    for g in range(first.shape[0] // CHUNK):
        pieces.append(first[g * CHUNK:(g + 1) * CHUNK])
        pieces.append(second[g * CHUNK:(g + 1) * CHUNK])
    return jnp.concatenate(pieces, axis=0)


def step_kernel(n_a, split_x, final, t_blk, src_ref, row_ref, kind_ref, ask_ref, *refs):
    a_refs = refs[:n_a]
    refs = refs[n_a:]
    if split_x:
        cura_ref, curb_ref, inca_ref, incb_ref = refs[:4]
        refs = refs[4:]
    else:
        cur_ref, inc_ref = refs[:2]
        refs = refs[2:]
    deg_ref, out_ref, side_ref, acc_ref = refs
    s = pl.program_id(0)
    last = pl.num_programs(0) - 1

    @pl.when(s == 0)
    def _():
        acc_ref[...] = jnp.zeros_like(acc_ref)

    def body(j, carry):
        t = s * t_blk + j
        r = row_ref[t]
        c = src_ref[t]
        rem = kind_ref[t] == 3
        cl = jnp.minimum(c, BLK_DEV - 1)
        if split_x:
            xa = jnp.where(rem, inca_ref[c], cura_ref[cl])
            xb = jnp.where(rem, incb_ref[c], curb_ref[cl])
            x = interleave(xa, xb)
        else:
            x = jnp.where(rem, inc_ref[c], cur_ref[cl])
        for p in range(n_a):
            acc_ref[r, p * HALF:(p + 1) * HALF, :] += jnp.dot(a_refs[p][j], x, preferred_element_type=jnp.float32)
        return carry

    lax.fori_loop(0, t_blk, body, 0, unroll=UNROLL)

    @pl.when(s == last)
    def _():
        deg_cols = deg_ref[...].T
        m = jnp.full((1, out_ref.shape[-1]), -jnp.inf, jnp.float32)
        for r in range(BLK_DEV):
            val = acc_ref[r] / deg_cols[:, r:r + 1]
            if n_a == 2:
                val = interleave(val[:HALF], val[HALF:])
            out_ref[r] = val.astype(out_ref.dtype)
            if final:
                m = jnp.maximum(m, jnp.max(val, axis=0, keepdims=True))
        if final:
            side_ref[...] = jnp.broadcast_to(m, side_ref.shape)
        else:
            def send(q, carry):
                side_ref[q] = out_ref[ask_ref[q]]
                return carry

            lax.fori_loop(0, side_ref.shape[0], send, 0)


def diffuse(a_parts, xs, deg, src, rows, kind, asked, final, t_blk):
    slots = a_parts[0].shape[0]
    genes = xs[0].shape[-1]
    n_a = len(a_parts)
    split_x = len(xs) == 4
    n_ask = asked.shape[0]
    out_rows = HALF * n_a

    def full(shape):
        return pl.BlockSpec(shape, lambda s, *_: (0,) * len(shape), pipeline_mode=pl.Buffered(1))

    in_specs = [pl.BlockSpec((t_blk, HALF, BS), lambda s, *_: (s, 0, 0)) for _ in a_parts]
    in_specs += [full(x.shape) for x in xs]
    in_specs.append(full(deg.shape))
    out_block = pl.BlockSpec((BLK_DEV, out_rows, genes), lambda s, *_: (0, 0, 0))
    if final:
        out_specs = [out_block, pl.BlockSpec((8, genes), lambda s, *_: (0, 0))]
        out_shape = [
            jax.ShapeDtypeStruct((BLK_DEV, out_rows, genes), jnp.float32),
            jax.ShapeDtypeStruct((8, genes), jnp.float32),
        ]
    else:
        out_specs = [out_block, pl.BlockSpec((n_ask, out_rows, genes), lambda s, *_: (0, 0, 0))]
        out_shape = [
            jax.ShapeDtypeStruct((BLK_DEV, out_rows, genes), jnp.bfloat16),
            jax.ShapeDtypeStruct((n_ask, out_rows, genes), jnp.bfloat16),
        ]
    grid_spec = pltpu.PrefetchScalarGridSpec(
        num_scalar_prefetch=4,
        grid=(slots // t_blk,),
        in_specs=in_specs,
        out_specs=out_specs,
        scratch_shapes=[pltpu.VMEM((BLK_DEV + 1, out_rows, genes), jnp.float32)],
    )
    return pl.pallas_call(
        functools.partial(step_kernel, n_a, split_x, final, t_blk),
        grid_spec=grid_spec,
        out_shape=out_shape,
        compiler_params=pltpu.CompilerParams(
            dimension_semantics=("arbitrary",), vmem_limit_bytes=60 * 1024 * 1024
        ),
    )(src, rows, kind, asked, *a_parts, *xs, deg)


def on_device(expression, affinity, tile_rows, tile_cols, tile_count):
    me = lax.axis_index("cell")
    gi = lax.axis_index("gene")
    peers = lax.axis_size("cell")
    n_gene = lax.axis_size("gene")
    genes = expression.shape[1]
    part_rows = affinity.shape[1]
    slots = affinity.shape[0]
    order = jnp.arange(slots, dtype=jnp.int32)
    valid = order < tile_count[0]
    local_row = tile_rows - me * BLK_DEV
    row_index = jnp.clip(jnp.where(valid, local_row, 0), 0, BLK_DEV - 1)
    junk_row = jnp.where(valid, row_index, BLK_DEV).astype(jnp.int32)
    used = min(slots, BLK_DEV + (peers - 1) * REQ_CAP)
    t_blk = max(d for d in range(1, 33) if used % d == 0)
    owner = tile_cols // BLK_DEV
    col_slot = tile_cols - owner * BLK_DEV
    remote = valid & (owner != me)
    selfish = valid & (tile_rows == tile_cols)

    diag = (
        lax.broadcasted_iota(jnp.int32, (part_rows, BS), 0) + gi * part_rows
        == lax.broadcasted_iota(jnp.int32, (part_rows, BS), 1)
    )
    keep = valid[:used, None, None] & jnp.logical_not(selfish[:used, None, None] & diag[None])
    masked = jnp.where(keep, affinity[:used], jnp.zeros_like(affinity[:used]))
    sub = part_rows // 2
    a_sets = [
        lax.all_gather(masked[:, h * sub:(h + 1) * sub], "gene", axis=1, tiled=True) for h in range(2)
    ]
    part_sums = jnp.sum(masked, axis=-1, dtype=jnp.float32)
    part_deg = jax.ops.segment_sum(part_sums, row_index[:used], BLK_DEV)
    deg = lax.all_gather(part_deg, "gene", axis=1, tiled=True)
    deg_sets = deg.reshape(BLK_DEV, n_gene, 2, sub)
    deg_a = deg_sets[:, :, 0].reshape(BLK_DEV, HALF)
    deg_b = deg_sets[:, :, 1].reshape(BLK_DEV, HALF)
    deg_ab = jnp.concatenate([deg_a, deg_b], axis=1)

    rank = ranks_of(owner, remote)
    peer_ids = jnp.arange(peers, dtype=jnp.int32)
    place = jnp.arange(REQ_CAP, dtype=jnp.int32)
    hit = (
        remote[:, None, None]
        & (owner[:, None, None] == peer_ids[None, :, None])
        & (rank[:, None, None] == place[None, None, :])
    )
    wanted = jnp.sum(jnp.where(hit, col_slot[:, None, None] + 1, 0), axis=0) - 1
    top_start = jnp.max(expression, axis=0).astype(jnp.float32)
    request = jnp.concatenate(
        [wanted.astype(jnp.float32), jnp.broadcast_to(top_start[None, :], (peers, genes))], axis=1
    )
    reply = lax.all_to_all(request, "cell", split_axis=0, concat_axis=0, tiled=True)
    asked = jnp.clip(reply[:, :REQ_CAP].astype(jnp.int32), 0, BLK_DEV - 1).reshape(-1)
    top_start = jnp.max(reply[:, REQ_CAP:], axis=0)

    kind = jnp.where(remote, 3, jnp.where(selfish, 2, jnp.where(valid, 1, 0))).astype(jnp.int32)
    src = jnp.where(remote, owner * REQ_CAP + rank, jnp.where(valid, col_slot, 0))
    src = jnp.where(remote, jnp.clip(src, 0, peers * REQ_CAP - 1), jnp.clip(src, 0, BLK_DEV - 1)).astype(jnp.int32)
    tables = (src, junk_row, kind, asked)

    def exchange(out, rows_):
        got = lax.all_to_all(
            out.reshape(peers, REQ_CAP, rows_, genes), "cell", split_axis=0, concat_axis=0, tiled=True
        )
        return got.reshape(peers * REQ_CAP, rows_, genes)

    x0 = expression.reshape(BLK_DEV, BS, genes)
    inc0 = exchange(x0[asked], BS)
    cur_a, side_a = diffuse([a_sets[0]], [x0, inc0], deg_a, *tables, False, t_blk)
    inc_a = exchange(side_a, HALF)
    cur_b, side_b = diffuse([a_sets[1]], [x0, inc0], deg_b, *tables, False, t_blk)
    inc_b = exchange(side_b, HALF)
    cur, side = diffuse(a_sets, [cur_a, cur_b, inc_a, inc_b], deg_ab, *tables, False, t_blk)
    inc = exchange(side, BS)
    last, side = diffuse(a_sets, [cur, inc], deg_ab, *tables, True, t_blk)
    last = last.reshape(BLK_DEV * BS, genes)
    top_end = side[0]
    top_end = jnp.max(
        lax.all_to_all(jnp.broadcast_to(top_end[None, :], (peers, genes)), "cell", 0, 0, tiled=True), axis=0
    )
    return last * (top_start / top_end)[None, :]


def solution(mesh):
    return jax.shard_map(
        on_device,
        mesh=mesh,
        in_specs=(P("cell", "gene"), P("cell", "gene", None), P("cell"), P("cell"), P("cell")),
        out_specs=P("cell", "gene"),
        check_vma=False,
    )
```

```python
import functools

import jax
import jax.numpy as jnp
from jax import lax
from jax.experimental import pallas as pl
from jax.experimental.pallas import tpu as pltpu
from jax.sharding import PartitionSpec as P

BS = 256
BLK_DEV = 32
REQ_CAP = 3
STEPS = 3
UNROLL = 5


def ranks_of(owner, remote):
    count = owner.shape[-1]
    order = jnp.arange(count, dtype=jnp.int32)
    earlier = order[None, :] < order[:, None]
    same = (owner[..., :, None] == owner[..., None, :]) & remote[..., None, :] & earlier
    return jnp.sum(same.astype(jnp.int32), axis=-1)


def interleave(first, second, n_gene):
    ca = first.shape[0] // n_gene
    cb = second.shape[0] // n_gene
    pieces = []
    for g in range(n_gene):
        pieces.append(first[g * ca:(g + 1) * ca])
        pieces.append(second[g * cb:(g + 1) * cb])
    return jnp.concatenate(pieces, axis=0)


def step_kernel(n_a, split_x, final, t_blk, n_gene, src_ref, row_ref, kind_ref, ask_ref, *refs):
    a_refs = refs[:n_a]
    refs = refs[n_a:]
    if split_x:
        cura_ref, curb_ref, inca_ref, incb_ref = refs[:4]
        refs = refs[4:]
    else:
        cur_ref, inc_ref = refs[:2]
        refs = refs[2:]
    deg_ref, out_ref, side_ref, acc_ref = refs
    s = pl.program_id(0)
    last = pl.num_programs(0) - 1

    @pl.when(s == 0)
    def _():
        acc_ref[...] = jnp.zeros_like(acc_ref)

    def body(j, carry):
        t = s * t_blk + j
        r = row_ref[t]
        c = src_ref[t]
        rem = kind_ref[t] == 3
        cl = jnp.minimum(c, BLK_DEV - 1)
        if split_x:
            xa = jnp.where(rem, inca_ref[c], cura_ref[cl])
            xb = jnp.where(rem, incb_ref[c], curb_ref[cl])
            x = interleave(xa, xb, n_gene)
        else:
            x = jnp.where(rem, inc_ref[c], cur_ref[cl])
        lo = 0
        for p in range(n_a):
            hi = lo + a_refs[p].shape[1]
            acc_ref[r, lo:hi, :] += jnp.dot(a_refs[p][j], x, preferred_element_type=jnp.float32)
            lo = hi
        return carry

    lax.fori_loop(0, t_blk, body, 0, unroll=UNROLL)

    @pl.when(s == last)
    def _():
        deg_cols = deg_ref[...].T
        m = jnp.full((1, out_ref.shape[-1]), -jnp.inf, jnp.float32)
        for r in range(BLK_DEV):
            val = acc_ref[r] / deg_cols[:, r:r + 1]
            if n_a == 2:
                ra = a_refs[0].shape[1]
                val = interleave(val[:ra], val[ra:], n_gene)
            out_ref[r] = val.astype(out_ref.dtype)
            if final:
                m = jnp.maximum(m, jnp.max(val, axis=0, keepdims=True))
        if final:
            side_ref[...] = jnp.broadcast_to(m, side_ref.shape)
        else:
            def send(q, carry):
                side_ref[q] = out_ref[ask_ref[q]]
                return carry

            lax.fori_loop(0, side_ref.shape[0], send, 0)


def diffuse(a_parts, xs, deg, src, rows, kind, asked, final, t_blk, n_gene):
    slots = a_parts[0].shape[0]
    genes = xs[0].shape[-1]
    n_a = len(a_parts)
    split_x = len(xs) == 4
    n_ask = asked.shape[0]
    out_rows = sum(a.shape[1] for a in a_parts)

    def full(shape):
        return pl.BlockSpec(shape, lambda s, *_: (0,) * len(shape), pipeline_mode=pl.Buffered(1))

    in_specs = [pl.BlockSpec((t_blk, a.shape[1], BS), lambda s, *_: (s, 0, 0)) for a in a_parts]
    in_specs += [full(x.shape) for x in xs]
    in_specs.append(full(deg.shape))
    out_block = pl.BlockSpec((BLK_DEV, out_rows, genes), lambda s, *_: (0, 0, 0))
    if final:
        out_specs = [out_block, pl.BlockSpec((8, genes), lambda s, *_: (0, 0))]
        out_shape = [
            jax.ShapeDtypeStruct((BLK_DEV, out_rows, genes), jnp.float32),
            jax.ShapeDtypeStruct((8, genes), jnp.float32),
        ]
    else:
        out_specs = [out_block, pl.BlockSpec((n_ask, out_rows, genes), lambda s, *_: (0, 0, 0))]
        out_shape = [
            jax.ShapeDtypeStruct((BLK_DEV, out_rows, genes), jnp.bfloat16),
            jax.ShapeDtypeStruct((n_ask, out_rows, genes), jnp.bfloat16),
        ]
    grid_spec = pltpu.PrefetchScalarGridSpec(
        num_scalar_prefetch=4,
        grid=(slots // t_blk,),
        in_specs=in_specs,
        out_specs=out_specs,
        scratch_shapes=[pltpu.VMEM((BLK_DEV + 1, out_rows, genes), jnp.float32)],
    )
    return pl.pallas_call(
        functools.partial(step_kernel, n_a, split_x, final, t_blk, n_gene),
        grid_spec=grid_spec,
        out_shape=out_shape,
        compiler_params=pltpu.CompilerParams(
            dimension_semantics=("arbitrary",), vmem_limit_bytes=60 * 1024 * 1024
        ),
    )(src, rows, kind, asked, *a_parts, *xs, deg)


def on_device(expression, affinity, tile_rows, tile_cols, tile_count):
    me = lax.axis_index("cell")
    gi = lax.axis_index("gene")
    peers = lax.axis_size("cell")
    n_gene = lax.axis_size("gene")
    genes = expression.shape[1]
    part_rows = affinity.shape[1]
    slots = affinity.shape[0]
    order = jnp.arange(slots, dtype=jnp.int32)
    valid = order < tile_count[0]
    local_row = tile_rows - me * BLK_DEV
    row_index = jnp.clip(jnp.where(valid, local_row, 0), 0, BLK_DEV - 1)
    junk_row = jnp.where(valid, row_index, BLK_DEV).astype(jnp.int32)
    used = min(slots, BLK_DEV + (peers - 1) * REQ_CAP)
    t_blk = max(d for d in range(1, 33) if used % d == 0)
    owner = tile_cols // BLK_DEV
    col_slot = tile_cols - owner * BLK_DEV
    remote = valid & (owner != me)
    selfish = valid & (tile_rows == tile_cols)

    diag = (
        lax.broadcasted_iota(jnp.int32, (part_rows, BS), 0) + gi * part_rows
        == lax.broadcasted_iota(jnp.int32, (part_rows, BS), 1)
    )
    keep = valid[:used, None, None] & jnp.logical_not(selfish[:used, None, None] & diag[None])
    masked = jnp.where(keep, affinity[:used], jnp.zeros_like(affinity[:used]))
    sub = 3 * part_rows // 4
    a_sets = [
        lax.all_gather(masked[:, :sub], "gene", axis=1, tiled=True),
        lax.all_gather(masked[:, sub:], "gene", axis=1, tiled=True),
    ]
    part_sums = jnp.sum(masked, axis=-1, dtype=jnp.float32)
    part_deg = jax.ops.segment_sum(part_sums, row_index[:used], BLK_DEV)
    deg = lax.all_gather(part_deg, "gene", axis=1, tiled=True)
    deg_sets = deg.reshape(BLK_DEV, n_gene, part_rows)
    deg_a = deg_sets[:, :, :sub].reshape(BLK_DEV, n_gene * sub)
    deg_b = deg_sets[:, :, sub:].reshape(BLK_DEV, n_gene * (part_rows - sub))
    deg_ab = jnp.concatenate([deg_a, deg_b], axis=1)

    rank = ranks_of(owner, remote)
    peer_ids = jnp.arange(peers, dtype=jnp.int32)
    place = jnp.arange(REQ_CAP, dtype=jnp.int32)
    hit = (
        remote[:, None, None]
        & (owner[:, None, None] == peer_ids[None, :, None])
        & (rank[:, None, None] == place[None, None, :])
    )
    wanted = jnp.sum(jnp.where(hit, col_slot[:, None, None] + 1, 0), axis=0) - 1
    top_start = jnp.max(expression, axis=0).astype(jnp.float32)
    request = jnp.concatenate(
        [wanted.astype(jnp.float32), jnp.broadcast_to(top_start[None, :], (peers, genes))], axis=1
    )
    reply = lax.all_to_all(request, "cell", split_axis=0, concat_axis=0, tiled=True)
    asked = jnp.clip(reply[:, :REQ_CAP].astype(jnp.int32), 0, BLK_DEV - 1).reshape(-1)
    top_start = jnp.max(reply[:, REQ_CAP:], axis=0)

    kind = jnp.where(remote, 3, jnp.where(selfish, 2, jnp.where(valid, 1, 0))).astype(jnp.int32)
    src = jnp.where(remote, owner * REQ_CAP + rank, jnp.where(valid, col_slot, 0))
    src = jnp.where(remote, jnp.clip(src, 0, peers * REQ_CAP - 1), jnp.clip(src, 0, BLK_DEV - 1)).astype(jnp.int32)
    tables = (src, junk_row, kind, asked)

    def exchange(out):
        rows_ = out.shape[1]
        got = lax.all_to_all(
            out.reshape(peers, REQ_CAP, rows_, genes), "cell", split_axis=0, concat_axis=0, tiled=True
        )
        return got.reshape(peers * REQ_CAP, rows_, genes)

    x0 = expression.reshape(BLK_DEV, BS, genes)
    inc0 = exchange(x0[asked])
    cur_a, side_a = diffuse([a_sets[0]], [x0, inc0], deg_a, *tables, False, t_blk, n_gene)
    inc_a = exchange(side_a)
    cur_b, side_b = diffuse([a_sets[1]], [x0, inc0], deg_b, *tables, False, t_blk, n_gene)
    inc_b = exchange(side_b)
    cur, side = diffuse(a_sets, [cur_a, cur_b, inc_a, inc_b], deg_ab, *tables, False, t_blk, n_gene)
    inc = exchange(side)
    last, side = diffuse(a_sets, [cur, inc], deg_ab, *tables, True, t_blk, n_gene)
    last = last.reshape(BLK_DEV * BS, genes)
    top_end = side[0]
    top_end = jnp.max(
        lax.all_to_all(jnp.broadcast_to(top_end[None, :], (peers, genes)), "cell", 0, 0, tiled=True), axis=0
    )
    return last * (top_start / top_end)[None, :]


def solution(mesh):
    return jax.shard_map(
        on_device,
        mesh=mesh,
        in_specs=(P("cell", "gene"), P("cell", "gene", None), P("cell"), P("cell"), P("cell")),
        out_specs=P("cell", "gene"),
        check_vma=False,
    )
```

```python
import functools

import jax
import jax.numpy as jnp
from jax import lax
from jax.experimental import pallas as pl
from jax.experimental.pallas import tpu as pltpu
from jax.sharding import PartitionSpec as P

BS = 256
BLK_DEV = 32
REQ_CAP = 3
STEPS = 3
UNROLL = 5


def ranks_of(owner, remote):
    count = owner.shape[-1]
    order = jnp.arange(count, dtype=jnp.int32)
    earlier = order[None, :] < order[:, None]
    same = (owner[..., :, None] == owner[..., None, :]) & remote[..., None, :] & earlier
    return jnp.sum(same.astype(jnp.int32), axis=-1)


def interleave(first, second, n_gene):
    ca = first.shape[0] // n_gene
    cb = second.shape[0] // n_gene
    pieces = []
    for g in range(n_gene):
        pieces.append(first[g * ca:(g + 1) * ca])
        pieces.append(second[g * cb:(g + 1) * cb])
    return jnp.concatenate(pieces, axis=0)


def step_kernel(n_a, split_x, final, t_blk, n_gene, src_ref, row_ref, kind_ref, ask_ref, *refs):
    a_refs = refs[:n_a]
    refs = refs[n_a:]
    if split_x:
        cura_ref, curb_ref, inca_ref, incb_ref = refs[:4]
        refs = refs[4:]
    else:
        cur_ref, inc_ref = refs[:2]
        refs = refs[2:]
    deg_ref, out_ref, side_ref, acc_ref = refs
    s = pl.program_id(0)
    last = pl.num_programs(0) - 1

    @pl.when(s == 0)
    def _():
        acc_ref[...] = jnp.zeros_like(acc_ref)

    def body(j, carry):
        t = s * t_blk + j
        r = row_ref[t]
        c = src_ref[t]
        rem = kind_ref[t] == 3
        cl = jnp.minimum(c, BLK_DEV - 1)
        if split_x:
            xa = jnp.where(rem, inca_ref[c], cura_ref[cl])
            xb = jnp.where(rem, incb_ref[c], curb_ref[cl])
            x = interleave(xa, xb, n_gene)
        else:
            x = jnp.where(rem, inc_ref[c], cur_ref[cl])
        lo = 0
        for p in range(n_a):
            hi = lo + a_refs[p].shape[1]
            acc_ref[r, lo:hi, :] += jnp.dot(a_refs[p][j], x, preferred_element_type=jnp.float32)
            lo = hi
        return carry

    lax.fori_loop(0, t_blk, body, 0, unroll=UNROLL)

    @pl.when(s == last)
    def _():
        deg_cols = deg_ref[...].T
        m = jnp.full((1, out_ref.shape[-1]), -jnp.inf, jnp.float32)
        for r in range(BLK_DEV):
            val = acc_ref[r] / deg_cols[:, r:r + 1]
            if n_a == 2:
                ra = a_refs[0].shape[1]
                val = interleave(val[:ra], val[ra:], n_gene)
            out_ref[r] = val.astype(out_ref.dtype)
            if final:
                m = jnp.maximum(m, jnp.max(val, axis=0, keepdims=True))
        if final:
            side_ref[...] = jnp.broadcast_to(m, side_ref.shape)
        else:
            def send(q, carry):
                side_ref[q] = out_ref[ask_ref[q]]
                return carry

            lax.fori_loop(0, side_ref.shape[0], send, 0)


def diffuse(a_parts, xs, deg, src, rows, kind, asked, final, t_blk, n_gene):
    slots = a_parts[0].shape[0]
    genes = xs[0].shape[-1]
    n_a = len(a_parts)
    split_x = len(xs) == 4
    n_ask = asked.shape[0]
    out_rows = sum(a.shape[1] for a in a_parts)

    def full(shape):
        return pl.BlockSpec(shape, lambda s, *_: (0,) * len(shape), pipeline_mode=pl.Buffered(1))

    in_specs = [pl.BlockSpec((t_blk, a.shape[1], BS), lambda s, *_: (s, 0, 0)) for a in a_parts]
    in_specs += [full(x.shape) for x in xs]
    in_specs.append(full(deg.shape))
    out_block = pl.BlockSpec((BLK_DEV, out_rows, genes), lambda s, *_: (0, 0, 0))
    if final:
        out_specs = [out_block, pl.BlockSpec((8, genes), lambda s, *_: (0, 0))]
        out_shape = [
            jax.ShapeDtypeStruct((BLK_DEV, out_rows, genes), jnp.float32),
            jax.ShapeDtypeStruct((8, genes), jnp.float32),
        ]
    else:
        out_specs = [out_block, pl.BlockSpec((n_ask, out_rows, genes), lambda s, *_: (0, 0, 0))]
        out_shape = [
            jax.ShapeDtypeStruct((BLK_DEV, out_rows, genes), jnp.bfloat16),
            jax.ShapeDtypeStruct((n_ask, out_rows, genes), jnp.bfloat16),
        ]
    grid_spec = pltpu.PrefetchScalarGridSpec(
        num_scalar_prefetch=4,
        grid=(slots // t_blk,),
        in_specs=in_specs,
        out_specs=out_specs,
        scratch_shapes=[pltpu.VMEM((BLK_DEV + 1, out_rows, genes), jnp.float32)],
    )
    return pl.pallas_call(
        functools.partial(step_kernel, n_a, split_x, final, t_blk, n_gene),
        grid_spec=grid_spec,
        out_shape=out_shape,
        compiler_params=pltpu.CompilerParams(
            dimension_semantics=("arbitrary",), vmem_limit_bytes=60 * 1024 * 1024
        ),
    )(src, rows, kind, asked, *a_parts, *xs, deg)


def on_device(expression, affinity, tile_rows, tile_cols, tile_count):
    me = lax.axis_index("cell")
    gi = lax.axis_index("gene")
    peers = lax.axis_size("cell")
    n_gene = lax.axis_size("gene")
    genes = expression.shape[1]
    part_rows = affinity.shape[1]
    slots = affinity.shape[0]
    order = jnp.arange(slots, dtype=jnp.int32)
    valid = order < tile_count[0]
    local_row = tile_rows - me * BLK_DEV
    row_index = jnp.clip(jnp.where(valid, local_row, 0), 0, BLK_DEV - 1)
    junk_row = jnp.where(valid, row_index, BLK_DEV).astype(jnp.int32)
    used = min(slots, BLK_DEV + (peers - 1) * REQ_CAP)
    t_blk = max(d for d in range(1, 33) if used % d == 0)
    owner = tile_cols // BLK_DEV
    col_slot = tile_cols - owner * BLK_DEV
    remote = valid & (owner != me)
    selfish = valid & (tile_rows == tile_cols)

    diag = (
        lax.broadcasted_iota(jnp.int32, (part_rows, BS), 0) + gi * part_rows
        == lax.broadcasted_iota(jnp.int32, (part_rows, BS), 1)
    )
    keep = valid[:used, None, None] & jnp.logical_not(selfish[:used, None, None] & diag[None])
    masked = jnp.where(keep, affinity[:used], jnp.zeros_like(affinity[:used]))
    sub = 3 * part_rows // 4
    first_set = lax.all_gather(masked[:, :sub], "gene", axis=1, tiled=True)
    first_set, rest = lax.optimization_barrier((first_set, masked[:, sub:]))
    a_sets = [first_set, lax.all_gather(rest, "gene", axis=1, tiled=True)]
    part_sums = jnp.sum(masked, axis=-1, dtype=jnp.float32)
    part_deg = jax.ops.segment_sum(part_sums, row_index[:used], BLK_DEV)
    deg = lax.all_gather(part_deg, "gene", axis=1, tiled=True)
    deg_sets = deg.reshape(BLK_DEV, n_gene, part_rows)
    deg_a = deg_sets[:, :, :sub].reshape(BLK_DEV, n_gene * sub)
    deg_b = deg_sets[:, :, sub:].reshape(BLK_DEV, n_gene * (part_rows - sub))
    deg_ab = jnp.concatenate([deg_a, deg_b], axis=1)

    rank = ranks_of(owner, remote)
    peer_ids = jnp.arange(peers, dtype=jnp.int32)
    place = jnp.arange(REQ_CAP, dtype=jnp.int32)
    hit = (
        remote[:, None, None]
        & (owner[:, None, None] == peer_ids[None, :, None])
        & (rank[:, None, None] == place[None, None, :])
    )
    wanted = jnp.sum(jnp.where(hit, col_slot[:, None, None] + 1, 0), axis=0) - 1
    top_start = jnp.max(expression, axis=0).astype(jnp.float32)
    request = jnp.concatenate(
        [wanted.astype(jnp.float32), jnp.broadcast_to(top_start[None, :], (peers, genes))], axis=1
    )
    reply = lax.all_to_all(request, "cell", split_axis=0, concat_axis=0, tiled=True)
    asked = jnp.clip(reply[:, :REQ_CAP].astype(jnp.int32), 0, BLK_DEV - 1).reshape(-1)
    top_start = jnp.max(reply[:, REQ_CAP:], axis=0)

    kind = jnp.where(remote, 3, jnp.where(selfish, 2, jnp.where(valid, 1, 0))).astype(jnp.int32)
    src = jnp.where(remote, owner * REQ_CAP + rank, jnp.where(valid, col_slot, 0))
    src = jnp.where(remote, jnp.clip(src, 0, peers * REQ_CAP - 1), jnp.clip(src, 0, BLK_DEV - 1)).astype(jnp.int32)
    tables = (src, junk_row, kind, asked)

    def exchange(out):
        rows_ = out.shape[1]
        got = lax.all_to_all(
            out.reshape(peers, REQ_CAP, rows_, genes), "cell", split_axis=0, concat_axis=0, tiled=True
        )
        return got.reshape(peers * REQ_CAP, rows_, genes)

    x0 = expression.reshape(BLK_DEV, BS, genes)
    inc0 = exchange(x0[asked])
    cur_a, side_a = diffuse([a_sets[0]], [x0, inc0], deg_a, *tables, False, t_blk, n_gene)
    inc_a = exchange(side_a)
    cur_b, side_b = diffuse([a_sets[1]], [x0, inc0], deg_b, *tables, False, t_blk, n_gene)
    inc_b = exchange(side_b)
    cur, side = diffuse(a_sets, [cur_a, cur_b, inc_a, inc_b], deg_ab, *tables, False, t_blk, n_gene)
    inc = exchange(side)
    last, side = diffuse(a_sets, [cur, inc], deg_ab, *tables, True, t_blk, n_gene)
    last = last.reshape(BLK_DEV * BS, genes)
    top_end = side[0]
    top_end = jnp.max(
        lax.all_to_all(jnp.broadcast_to(top_end[None, :], (peers, genes)), "cell", 0, 0, tiled=True), axis=0
    )
    return last * (top_start / top_end)[None, :]


def solution(mesh):
    return jax.shard_map(
        on_device,
        mesh=mesh,
        in_specs=(P("cell", "gene"), P("cell", "gene", None), P("cell"), P("cell"), P("cell")),
        out_specs=P("cell", "gene"),
        check_vma=False,
    )
```

```python
import functools

import jax
import jax.numpy as jnp
from jax import lax
from jax.experimental import pallas as pl
from jax.experimental.pallas import tpu as pltpu
from jax.sharding import PartitionSpec as P

BS = 256
BLK_DEV = 32
REQ_CAP = 3
STEPS = 3
UNROLL = 5
HALF = BS // 2
CHUNK = 32


def ranks_of(owner, remote):
    count = owner.shape[-1]
    order = jnp.arange(count, dtype=jnp.int32)
    earlier = order[None, :] < order[:, None]
    same = (owner[..., :, None] == owner[..., None, :]) & remote[..., None, :] & earlier
    return jnp.sum(same.astype(jnp.int32), axis=-1)


def interleave(first, second):
    pieces = []
    for g in range(first.shape[0] // CHUNK):
        pieces.append(first[g * CHUNK:(g + 1) * CHUNK])
        pieces.append(second[g * CHUNK:(g + 1) * CHUNK])
    return jnp.concatenate(pieces, axis=0)


def step_kernel(n_a, split_x, final, t_blk, src_ref, row_ref, kind_ref, ask_ref, *refs):
    a_refs = refs[:n_a]
    refs = refs[n_a:]
    if split_x:
        cura_ref, curb_ref, inca_ref, incb_ref = refs[:4]
        refs = refs[4:]
    else:
        cur_ref, inc_ref = refs[:2]
        refs = refs[2:]
    deg_ref, out_ref, side_ref, acc_ref = refs
    s = pl.program_id(0)
    last = pl.num_programs(0) - 1

    @pl.when(s == 0)
    def _():
        acc_ref[...] = jnp.zeros_like(acc_ref)

    def body(j, carry):
        t = s * t_blk + j
        r = row_ref[t]
        c = src_ref[t]
        rem = kind_ref[t] == 3
        cl = jnp.minimum(c, BLK_DEV - 1)
        if split_x:
            xa = jnp.where(rem, inca_ref[c], cura_ref[cl])
            xb = jnp.where(rem, incb_ref[c], curb_ref[cl])
            x = interleave(xa, xb)
        else:
            x = jnp.where(rem, inc_ref[c], cur_ref[cl])
        for p in range(n_a):
            acc_ref[r, p * HALF:(p + 1) * HALF, :] += jnp.dot(a_refs[p][j], x, preferred_element_type=jnp.float32)
        return carry

    lax.fori_loop(0, t_blk, body, 0, unroll=UNROLL)

    @pl.when(s == last)
    def _():
        deg_cols = deg_ref[...].T
        m = jnp.full((1, out_ref.shape[-1]), -jnp.inf, jnp.float32)
        for r in range(BLK_DEV):
            val = acc_ref[r] / deg_cols[:, r:r + 1]
            if n_a == 2:
                val = interleave(val[:HALF], val[HALF:])
            out_ref[r] = val.astype(out_ref.dtype)
            if final:
                m = jnp.maximum(m, jnp.max(val, axis=0, keepdims=True))
        if final:
            side_ref[...] = jnp.broadcast_to(m, side_ref.shape)
        else:
            def send(q, carry):
                side_ref[q] = out_ref[ask_ref[q]]
                return carry

            lax.fori_loop(0, side_ref.shape[0], send, 0)


def diffuse(a_parts, xs, deg, src, rows, kind, asked, final, t_blk):
    slots = a_parts[0].shape[0]
    genes = xs[0].shape[-1]
    n_a = len(a_parts)
    split_x = len(xs) == 4
    n_ask = asked.shape[0]
    out_rows = HALF * n_a

    def full(shape):
        return pl.BlockSpec(shape, lambda s, *_: (0,) * len(shape), pipeline_mode=pl.Buffered(1))

    in_specs = [pl.BlockSpec((t_blk, HALF, BS), lambda s, *_: (s, 0, 0)) for _ in a_parts]
    in_specs += [full(x.shape) for x in xs]
    in_specs.append(full(deg.shape))
    out_block = pl.BlockSpec((BLK_DEV, out_rows, genes), lambda s, *_: (0, 0, 0))
    if final:
        out_specs = [out_block, pl.BlockSpec((8, genes), lambda s, *_: (0, 0))]
        out_shape = [
            jax.ShapeDtypeStruct((BLK_DEV, out_rows, genes), jnp.float32),
            jax.ShapeDtypeStruct((8, genes), jnp.float32),
        ]
    else:
        out_specs = [out_block, pl.BlockSpec((n_ask, out_rows, genes), lambda s, *_: (0, 0, 0))]
        out_shape = [
            jax.ShapeDtypeStruct((BLK_DEV, out_rows, genes), jnp.bfloat16),
            jax.ShapeDtypeStruct((n_ask, out_rows, genes), jnp.bfloat16),
        ]
    grid_spec = pltpu.PrefetchScalarGridSpec(
        num_scalar_prefetch=4,
        grid=(slots // t_blk,),
        in_specs=in_specs,
        out_specs=out_specs,
        scratch_shapes=[pltpu.VMEM((BLK_DEV + 1, out_rows, genes), jnp.float32)],
    )
    return pl.pallas_call(
        functools.partial(step_kernel, n_a, split_x, final, t_blk),
        grid_spec=grid_spec,
        out_shape=out_shape,
        compiler_params=pltpu.CompilerParams(
            dimension_semantics=("arbitrary",), vmem_limit_bytes=60 * 1024 * 1024
        ),
    )(src, rows, kind, asked, *a_parts, *xs, deg)


def on_device(expression, affinity, tile_rows, tile_cols, tile_count):
    me = lax.axis_index("cell")
    gi = lax.axis_index("gene")
    peers = lax.axis_size("cell")
    n_gene = lax.axis_size("gene")
    genes = expression.shape[1]
    part_rows = affinity.shape[1]
    slots = affinity.shape[0]
    order = jnp.arange(slots, dtype=jnp.int32)
    valid = order < tile_count[0]
    local_row = tile_rows - me * BLK_DEV
    row_index = jnp.clip(jnp.where(valid, local_row, 0), 0, BLK_DEV - 1)
    junk_row = jnp.where(valid, row_index, BLK_DEV).astype(jnp.int32)
    used = min(slots, BLK_DEV + (peers - 1) * REQ_CAP)
    t_blk = max(d for d in range(1, 33) if used % d == 0)
    owner = tile_cols // BLK_DEV
    col_slot = tile_cols - owner * BLK_DEV
    remote = valid & (owner != me)
    selfish = valid & (tile_rows == tile_cols)

    diag = (
        lax.broadcasted_iota(jnp.int32, (part_rows, BS), 0) + gi * part_rows
        == lax.broadcasted_iota(jnp.int32, (part_rows, BS), 1)
    )
    sub = part_rows // 2

    def set_part(h):
        d = diag[h * sub:(h + 1) * sub]
        keep = valid[:used, None, None] & jnp.logical_not(selfish[:used, None, None] & d[None])
        a = affinity[:used, h * sub:(h + 1) * sub]
        return jnp.where(keep, a, jnp.zeros_like(a))

    set_parts = [set_part(h) for h in range(2)]
    a_sets = [lax.all_gather(p, "gene", axis=1, tiled=True) for p in set_parts]
    part_sums = jnp.concatenate([jnp.sum(p, axis=-1, dtype=jnp.float32) for p in set_parts], axis=1)
    part_deg = jax.ops.segment_sum(part_sums, row_index[:used], BLK_DEV)
    deg = lax.all_gather(part_deg, "gene", axis=1, tiled=True)
    deg_sets = deg.reshape(BLK_DEV, n_gene, 2, sub)
    deg_a = deg_sets[:, :, 0].reshape(BLK_DEV, HALF)
    deg_b = deg_sets[:, :, 1].reshape(BLK_DEV, HALF)
    deg_ab = jnp.concatenate([deg_a, deg_b], axis=1)

    rank = ranks_of(owner, remote)
    peer_ids = jnp.arange(peers, dtype=jnp.int32)
    place = jnp.arange(REQ_CAP, dtype=jnp.int32)
    hit = (
        remote[:, None, None]
        & (owner[:, None, None] == peer_ids[None, :, None])
        & (rank[:, None, None] == place[None, None, :])
    )
    wanted = jnp.sum(jnp.where(hit, col_slot[:, None, None] + 1, 0), axis=0) - 1
    top_start = jnp.max(expression, axis=0).astype(jnp.float32)
    request = jnp.concatenate(
        [wanted.astype(jnp.float32), jnp.broadcast_to(top_start[None, :], (peers, genes))], axis=1
    )
    reply = lax.all_to_all(request, "cell", split_axis=0, concat_axis=0, tiled=True)
    asked = jnp.clip(reply[:, :REQ_CAP].astype(jnp.int32), 0, BLK_DEV - 1).reshape(-1)
    top_start = jnp.max(reply[:, REQ_CAP:], axis=0)

    kind = jnp.where(remote, 3, jnp.where(selfish, 2, jnp.where(valid, 1, 0))).astype(jnp.int32)
    src = jnp.where(remote, owner * REQ_CAP + rank, jnp.where(valid, col_slot, 0))
    src = jnp.where(remote, jnp.clip(src, 0, peers * REQ_CAP - 1), jnp.clip(src, 0, BLK_DEV - 1)).astype(jnp.int32)
    tables = (src, junk_row, kind, asked)

    def exchange(out, rows_):
        got = lax.all_to_all(
            out.reshape(peers, REQ_CAP, rows_, genes), "cell", split_axis=0, concat_axis=0, tiled=True
        )
        return got.reshape(peers * REQ_CAP, rows_, genes)

    x0 = expression.reshape(BLK_DEV, BS, genes)
    inc0 = exchange(x0[asked], BS)
    cur_a, side_a = diffuse([a_sets[0]], [x0, inc0], deg_a, *tables, False, t_blk)
    inc_a = exchange(side_a, HALF)
    cur_b, side_b = diffuse([a_sets[1]], [x0, inc0], deg_b, *tables, False, t_blk)
    inc_b = exchange(side_b, HALF)
    cur, side = diffuse(a_sets, [cur_a, cur_b, inc_a, inc_b], deg_ab, *tables, False, t_blk)
    inc = exchange(side, BS)
    last, side = diffuse(a_sets, [cur, inc], deg_ab, *tables, True, t_blk)
    last = last.reshape(BLK_DEV * BS, genes)
    top_end = side[0]
    top_end = jnp.max(
        lax.all_to_all(jnp.broadcast_to(top_end[None, :], (peers, genes)), "cell", 0, 0, tiled=True), axis=0
    )
    return last * (top_start / top_end)[None, :]


def solution(mesh):
    return jax.shard_map(
        on_device,
        mesh=mesh,
        in_specs=(P("cell", "gene"), P("cell", "gene", None), P("cell"), P("cell"), P("cell")),
        out_specs=P("cell", "gene"),
        check_vma=False,
    )
```

```python
import functools

import jax
import jax.numpy as jnp
from jax import lax
from jax.experimental import pallas as pl
from jax.experimental.pallas import tpu as pltpu
from jax.sharding import PartitionSpec as P

BS = 256
BLK_DEV = 32
REQ_CAP = 3
STEPS = 3
UNROLL = 5
HALF = BS // 2
CHUNK = 32


def ranks_of(owner, remote):
    count = owner.shape[-1]
    order = jnp.arange(count, dtype=jnp.int32)
    earlier = order[None, :] < order[:, None]
    same = (owner[..., :, None] == owner[..., None, :]) & remote[..., None, :] & earlier
    return jnp.sum(same.astype(jnp.int32), axis=-1)


def interleave(first, second):
    pieces = []
    for g in range(first.shape[0] // CHUNK):
        pieces.append(first[g * CHUNK:(g + 1) * CHUNK])
        pieces.append(second[g * CHUNK:(g + 1) * CHUNK])
    return jnp.concatenate(pieces, axis=0)


def step_kernel(n_a, split_x, final, t_blk, src_ref, row_ref, kind_ref, ask_ref, *refs):
    a_refs = refs[:n_a]
    refs = refs[n_a:]
    if split_x:
        cura_ref, curb_ref, inca_ref, incb_ref = refs[:4]
        refs = refs[4:]
    else:
        cur_ref, inc_ref = refs[:2]
        refs = refs[2:]
    deg_ref, out_ref, side_ref, acc_ref = refs
    s = pl.program_id(0)
    last = pl.num_programs(0) - 1

    @pl.when(s == 0)
    def _():
        acc_ref[...] = jnp.zeros_like(acc_ref)

    def body(j, carry):
        t = s * t_blk + j
        r = row_ref[t]
        c = src_ref[t]
        rem = kind_ref[t] == 3
        cl = jnp.minimum(c, BLK_DEV - 1)
        if split_x:
            xa = jnp.where(rem, inca_ref[c], cura_ref[cl])
            xb = jnp.where(rem, incb_ref[c], curb_ref[cl])
            x = interleave(xa, xb)
        else:
            x = jnp.where(rem, inc_ref[c], cur_ref[cl])
        for p in range(n_a):
            acc_ref[r, p * HALF:(p + 1) * HALF, :] += jnp.dot(a_refs[p][j], x, preferred_element_type=jnp.float32)
        return carry

    lax.fori_loop(0, t_blk, body, 0, unroll=UNROLL)

    @pl.when(s == last)
    def _():
        deg_cols = deg_ref[...].T
        m = jnp.full((1, out_ref.shape[-1]), -jnp.inf, jnp.float32)
        for r in range(BLK_DEV):
            val = acc_ref[r] / deg_cols[:, r:r + 1]
            if n_a == 2:
                val = interleave(val[:HALF], val[HALF:])
            out_ref[r] = val.astype(out_ref.dtype)
            if final:
                m = jnp.maximum(m, jnp.max(val, axis=0, keepdims=True))
        if final:
            side_ref[...] = jnp.broadcast_to(m, side_ref.shape)
        else:
            def send(q, carry):
                side_ref[q] = out_ref[ask_ref[q]]
                return carry

            lax.fori_loop(0, side_ref.shape[0], send, 0)


def diffuse(a_parts, xs, deg, src, rows, kind, asked, final, t_blk):
    slots = a_parts[0].shape[0]
    genes = xs[0].shape[-1]
    n_a = len(a_parts)
    split_x = len(xs) == 4
    n_ask = asked.shape[0]
    out_rows = HALF * n_a

    def full(shape):
        return pl.BlockSpec(shape, lambda s, *_: (0,) * len(shape), pipeline_mode=pl.Buffered(1))

    in_specs = [pl.BlockSpec((t_blk, HALF, BS), lambda s, *_: (s, 0, 0)) for _ in a_parts]
    in_specs += [full(x.shape) for x in xs]
    in_specs.append(full(deg.shape))
    out_block = pl.BlockSpec((BLK_DEV, out_rows, genes), lambda s, *_: (0, 0, 0))
    if final:
        out_specs = [out_block, pl.BlockSpec((8, genes), lambda s, *_: (0, 0))]
        out_shape = [
            jax.ShapeDtypeStruct((BLK_DEV, out_rows, genes), jnp.float32),
            jax.ShapeDtypeStruct((8, genes), jnp.float32),
        ]
    else:
        out_specs = [out_block, pl.BlockSpec((n_ask, out_rows, genes), lambda s, *_: (0, 0, 0))]
        out_shape = [
            jax.ShapeDtypeStruct((BLK_DEV, out_rows, genes), jnp.bfloat16),
            jax.ShapeDtypeStruct((n_ask, out_rows, genes), jnp.bfloat16),
        ]
    grid_spec = pltpu.PrefetchScalarGridSpec(
        num_scalar_prefetch=4,
        grid=(slots // t_blk,),
        in_specs=in_specs,
        out_specs=out_specs,
        scratch_shapes=[pltpu.VMEM((BLK_DEV + 1, out_rows, genes), jnp.float32)],
    )
    return pl.pallas_call(
        functools.partial(step_kernel, n_a, split_x, final, t_blk),
        grid_spec=grid_spec,
        out_shape=out_shape,
        compiler_params=pltpu.CompilerParams(
            dimension_semantics=("arbitrary",), vmem_limit_bytes=60 * 1024 * 1024
        ),
    )(src, rows, kind, asked, *a_parts, *xs, deg)


def on_device(expression, affinity, tile_rows, tile_cols, tile_count):
    me = lax.axis_index("cell")
    gi = lax.axis_index("gene")
    peers = lax.axis_size("cell")
    n_gene = lax.axis_size("gene")
    genes = expression.shape[1]
    part_rows = affinity.shape[1]
    slots = affinity.shape[0]
    order = jnp.arange(slots, dtype=jnp.int32)
    valid = order < tile_count[0]
    local_row = tile_rows - me * BLK_DEV
    row_index = jnp.clip(jnp.where(valid, local_row, 0), 0, BLK_DEV - 1)
    junk_row = jnp.where(valid, row_index, BLK_DEV).astype(jnp.int32)
    used = min(slots, BLK_DEV + (peers - 1) * REQ_CAP)
    t_blk = max(d for d in range(1, 33) if used % d == 0)
    owner = tile_cols // BLK_DEV
    col_slot = tile_cols - owner * BLK_DEV
    remote = valid & (owner != me)
    selfish = valid & (tile_rows == tile_cols)

    diag = (
        lax.broadcasted_iota(jnp.int32, (part_rows, BS), 0) + gi * part_rows
        == lax.broadcasted_iota(jnp.int32, (part_rows, BS), 1)
    )
    sub = part_rows // 2

    def set_part(h):
        d = diag[h * sub:(h + 1) * sub]
        keep = valid[:used, None, None] & jnp.logical_not(selfish[:used, None, None] & d[None])
        a = affinity[:used, h * sub:(h + 1) * sub]
        return jnp.where(keep, a, jnp.zeros_like(a))

    set_parts = [set_part(h) for h in range(2)]
    a_sets = [lax.all_gather(p, "gene", axis=1, tiled=True) for p in set_parts]
    aff_sums = lax.optimization_barrier(affinity[:used])
    keep_all = valid[:used, None, None] & jnp.logical_not(selfish[:used, None, None] & diag[None])
    part_sums = jnp.sum(jnp.where(keep_all, aff_sums, jnp.zeros_like(aff_sums)), axis=-1, dtype=jnp.float32)
    part_deg = jax.ops.segment_sum(part_sums, row_index[:used], BLK_DEV)
    deg = lax.all_gather(part_deg, "gene", axis=1, tiled=True)
    deg_sets = deg.reshape(BLK_DEV, n_gene, 2, sub)
    deg_a = deg_sets[:, :, 0].reshape(BLK_DEV, HALF)
    deg_b = deg_sets[:, :, 1].reshape(BLK_DEV, HALF)
    deg_ab = jnp.concatenate([deg_a, deg_b], axis=1)

    rank = ranks_of(owner, remote)
    peer_ids = jnp.arange(peers, dtype=jnp.int32)
    place = jnp.arange(REQ_CAP, dtype=jnp.int32)
    hit = (
        remote[:, None, None]
        & (owner[:, None, None] == peer_ids[None, :, None])
        & (rank[:, None, None] == place[None, None, :])
    )
    wanted = jnp.sum(jnp.where(hit, col_slot[:, None, None] + 1, 0), axis=0) - 1
    top_start = jnp.max(expression, axis=0).astype(jnp.float32)
    request = jnp.concatenate(
        [wanted.astype(jnp.float32), jnp.broadcast_to(top_start[None, :], (peers, genes))], axis=1
    )
    reply = lax.all_to_all(request, "cell", split_axis=0, concat_axis=0, tiled=True)
    asked = jnp.clip(reply[:, :REQ_CAP].astype(jnp.int32), 0, BLK_DEV - 1).reshape(-1)
    top_start = jnp.max(reply[:, REQ_CAP:], axis=0)

    kind = jnp.where(remote, 3, jnp.where(selfish, 2, jnp.where(valid, 1, 0))).astype(jnp.int32)
    src = jnp.where(remote, owner * REQ_CAP + rank, jnp.where(valid, col_slot, 0))
    src = jnp.where(remote, jnp.clip(src, 0, peers * REQ_CAP - 1), jnp.clip(src, 0, BLK_DEV - 1)).astype(jnp.int32)
    tables = (src, junk_row, kind, asked)

    def exchange(out, rows_):
        got = lax.all_to_all(
            out.reshape(peers, REQ_CAP, rows_, genes), "cell", split_axis=0, concat_axis=0, tiled=True
        )
        return got.reshape(peers * REQ_CAP, rows_, genes)

    x0 = expression.reshape(BLK_DEV, BS, genes)
    inc0 = exchange(x0[asked], BS)
    cur_a, side_a = diffuse([a_sets[0]], [x0, inc0], deg_a, *tables, False, t_blk)
    inc_a = exchange(side_a, HALF)
    cur_b, side_b = diffuse([a_sets[1]], [x0, inc0], deg_b, *tables, False, t_blk)
    inc_b = exchange(side_b, HALF)
    cur, side = diffuse(a_sets, [cur_a, cur_b, inc_a, inc_b], deg_ab, *tables, False, t_blk)
    inc = exchange(side, BS)
    last, side = diffuse(a_sets, [cur, inc], deg_ab, *tables, True, t_blk)
    last = last.reshape(BLK_DEV * BS, genes)
    top_end = side[0]
    top_end = jnp.max(
        lax.all_to_all(jnp.broadcast_to(top_end[None, :], (peers, genes)), "cell", 0, 0, tiled=True), axis=0
    )
    return last * (top_start / top_end)[None, :]


def solution(mesh):
    return jax.shard_map(
        on_device,
        mesh=mesh,
        in_specs=(P("cell", "gene"), P("cell", "gene", None), P("cell"), P("cell"), P("cell")),
        out_specs=P("cell", "gene"),
        check_vma=False,
    )
```

```python
import functools

import jax
import jax.numpy as jnp
from jax import lax
from jax.experimental import pallas as pl
from jax.experimental.pallas import tpu as pltpu
from jax.sharding import PartitionSpec as P

BS = 256
BLK_DEV = 32
REQ_CAP = 3
STEPS = 3
UNROLL = 5
HALF = BS // 2
CHUNK = 32


def ranks_of(owner, remote):
    count = owner.shape[-1]
    order = jnp.arange(count, dtype=jnp.int32)
    earlier = order[None, :] < order[:, None]
    same = (owner[..., :, None] == owner[..., None, :]) & remote[..., None, :] & earlier
    return jnp.sum(same.astype(jnp.int32), axis=-1)


def interleave(first, second):
    pieces = []
    for g in range(first.shape[0] // CHUNK):
        pieces.append(first[g * CHUNK:(g + 1) * CHUNK])
        pieces.append(second[g * CHUNK:(g + 1) * CHUNK])
    return jnp.concatenate(pieces, axis=0)


def step_kernel(n_a, split_x, final, t_blk, src_ref, row_ref, kind_ref, ask_ref, *refs):
    a_refs = refs[:n_a]
    refs = refs[n_a:]
    if split_x:
        cura_ref, curb_ref, inca_ref, incb_ref = refs[:4]
        refs = refs[4:]
    else:
        cur_ref, inc_ref = refs[:2]
        refs = refs[2:]
    deg_ref, out_ref, side_ref, acc_ref = refs
    s = pl.program_id(0)
    last = pl.num_programs(0) - 1

    @pl.when(s == 0)
    def _():
        acc_ref[...] = jnp.zeros_like(acc_ref)

    def body(j, carry):
        t = s * t_blk + j
        r = row_ref[t]
        c = src_ref[t]
        rem = kind_ref[t] == 3
        cl = jnp.minimum(c, BLK_DEV - 1)
        if split_x:
            xa = jnp.where(rem, inca_ref[c], cura_ref[cl])
            xb = jnp.where(rem, incb_ref[c], curb_ref[cl])
            x = interleave(xa, xb)
        else:
            x = jnp.where(rem, inc_ref[c], cur_ref[cl])
        for p in range(n_a):
            acc_ref[r, p * HALF:(p + 1) * HALF, :] += jnp.dot(a_refs[p][j], x, preferred_element_type=jnp.float32)
        return carry

    lax.fori_loop(0, t_blk, body, 0, unroll=UNROLL)

    @pl.when(s == last)
    def _():
        deg_cols = deg_ref[...].T
        m = jnp.full((1, out_ref.shape[-1]), -jnp.inf, jnp.float32)
        for r in range(BLK_DEV):
            val = acc_ref[r] / deg_cols[:, r:r + 1]
            if n_a == 2:
                val = interleave(val[:HALF], val[HALF:])
            out_ref[r] = val.astype(out_ref.dtype)
            if final:
                m = jnp.maximum(m, jnp.max(val, axis=0, keepdims=True))
        if final:
            side_ref[...] = jnp.broadcast_to(m, side_ref.shape)
        else:
            def send(q, carry):
                side_ref[q] = out_ref[ask_ref[q]]
                return carry

            lax.fori_loop(0, side_ref.shape[0], send, 0)


def diffuse(a_parts, xs, deg, src, rows, kind, asked, final, t_blk):
    slots = a_parts[0].shape[0]
    genes = xs[0].shape[-1]
    n_a = len(a_parts)
    split_x = len(xs) == 4
    n_ask = asked.shape[0]
    out_rows = HALF * n_a

    def full(shape):
        return pl.BlockSpec(shape, lambda s, *_: (0,) * len(shape), pipeline_mode=pl.Buffered(1))

    in_specs = [pl.BlockSpec((t_blk, HALF, BS), lambda s, *_: (s, 0, 0)) for _ in a_parts]
    in_specs += [full(x.shape) for x in xs]
    in_specs.append(full(deg.shape))
    out_block = pl.BlockSpec((BLK_DEV, out_rows, genes), lambda s, *_: (0, 0, 0))
    if final:
        out_specs = [out_block, pl.BlockSpec((8, genes), lambda s, *_: (0, 0))]
        out_shape = [
            jax.ShapeDtypeStruct((BLK_DEV, out_rows, genes), jnp.float32),
            jax.ShapeDtypeStruct((8, genes), jnp.float32),
        ]
    else:
        out_specs = [out_block, pl.BlockSpec((n_ask, out_rows, genes), lambda s, *_: (0, 0, 0))]
        out_shape = [
            jax.ShapeDtypeStruct((BLK_DEV, out_rows, genes), jnp.bfloat16),
            jax.ShapeDtypeStruct((n_ask, out_rows, genes), jnp.bfloat16),
        ]
    grid_spec = pltpu.PrefetchScalarGridSpec(
        num_scalar_prefetch=4,
        grid=(slots // t_blk,),
        in_specs=in_specs,
        out_specs=out_specs,
        scratch_shapes=[pltpu.VMEM((BLK_DEV + 1, out_rows, genes), jnp.float32)],
    )
    return pl.pallas_call(
        functools.partial(step_kernel, n_a, split_x, final, t_blk),
        grid_spec=grid_spec,
        out_shape=out_shape,
        compiler_params=pltpu.CompilerParams(
            dimension_semantics=("arbitrary",), vmem_limit_bytes=60 * 1024 * 1024
        ),
    )(src, rows, kind, asked, *a_parts, *xs, deg)


def on_device(expression, affinity, tile_rows, tile_cols, tile_count):
    me = lax.axis_index("cell")
    gi = lax.axis_index("gene")
    peers = lax.axis_size("cell")
    n_gene = lax.axis_size("gene")
    genes = expression.shape[1]
    part_rows = affinity.shape[1]
    slots = affinity.shape[0]
    order = jnp.arange(slots, dtype=jnp.int32)
    valid = order < tile_count[0]
    local_row = tile_rows - me * BLK_DEV
    row_index = jnp.clip(jnp.where(valid, local_row, 0), 0, BLK_DEV - 1)
    junk_row = jnp.where(valid, row_index, BLK_DEV).astype(jnp.int32)
    used = min(slots, BLK_DEV + (peers - 1) * REQ_CAP)
    t_blk = max(d for d in range(1, 33) if used % d == 0)
    owner = tile_cols // BLK_DEV
    col_slot = tile_cols - owner * BLK_DEV
    remote = valid & (owner != me)
    selfish = valid & (tile_rows == tile_cols)

    diag = (
        lax.broadcasted_iota(jnp.int32, (part_rows, BS), 0) + gi * part_rows
        == lax.broadcasted_iota(jnp.int32, (part_rows, BS), 1)
    )
    sub = part_rows // 2

    def set_part(h):
        d = diag[h * sub:(h + 1) * sub]
        keep = valid[:used, None, None] & jnp.logical_not(selfish[:used, None, None] & d[None])
        a = affinity[:used, h * sub:(h + 1) * sub]
        return jnp.where(keep, a, jnp.zeros_like(a))

    set_parts = [set_part(h) for h in range(2)]
    a_sets = [lax.all_gather(p, "gene", axis=1, tiled=True) for p in set_parts]
    aff_sums = lax.optimization_barrier(affinity[:used])
    keep_all = valid[:used, None, None] & jnp.logical_not(selfish[:used, None, None] & diag[None])
    part_sums = jnp.sum(jnp.where(keep_all, aff_sums, jnp.zeros_like(aff_sums)), axis=-1, dtype=jnp.float32)
    part_deg = jax.ops.segment_sum(part_sums, row_index[:used], BLK_DEV)
    deg = lax.all_gather(part_deg, "gene", axis=1, tiled=True)
    deg_sets = deg.reshape(BLK_DEV, n_gene, 2, sub)
    deg_a = deg_sets[:, :, 0].reshape(BLK_DEV, HALF)
    deg_b = deg_sets[:, :, 1].reshape(BLK_DEV, HALF)
    deg_ab = jnp.concatenate([deg_a, deg_b], axis=1)

    rank = ranks_of(owner, remote)
    peer_ids = jnp.arange(peers, dtype=jnp.int32)
    place = jnp.arange(REQ_CAP, dtype=jnp.int32)
    hit = (
        remote[:, None, None]
        & (owner[:, None, None] == peer_ids[None, :, None])
        & (rank[:, None, None] == place[None, None, :])
    )
    wanted = jnp.sum(jnp.where(hit, col_slot[:, None, None] + 1, 0), axis=0) - 1
    top_start = jnp.max(expression, axis=0).astype(jnp.float32)
    request = jnp.concatenate(
        [wanted.astype(jnp.float32), jnp.broadcast_to(top_start[None, :], (peers, genes))], axis=1
    )
    reply = lax.all_to_all(request, "cell", split_axis=0, concat_axis=0, tiled=True)
    asked = jnp.clip(reply[:, :REQ_CAP].astype(jnp.int32), 0, BLK_DEV - 1).reshape(-1)
    top_start = jnp.max(reply[:, REQ_CAP:], axis=0)

    kind = jnp.where(remote, 3, jnp.where(selfish, 2, jnp.where(valid, 1, 0))).astype(jnp.int32)
    src = jnp.where(remote, owner * REQ_CAP + rank, jnp.where(valid, col_slot, 0))
    src = jnp.where(remote, jnp.clip(src, 0, peers * REQ_CAP - 1), jnp.clip(src, 0, BLK_DEV - 1)).astype(jnp.int32)
    tables = (src, junk_row, kind, asked)

    def exchange(out, rows_):
        got = lax.all_to_all(
            out.reshape(peers, REQ_CAP, rows_, genes), "cell", split_axis=0, concat_axis=0, tiled=True
        )
        return got.reshape(peers * REQ_CAP, rows_, genes)

    x0 = expression.reshape(BLK_DEV, BS, genes)
    inc0 = exchange(x0[asked], BS)
    cur_a, side_a = diffuse([a_sets[0]], [x0, inc0], deg_a, *tables, False, t_blk)
    inc_a = exchange(side_a, HALF)
    cur_b, side_b = diffuse([a_sets[1]], [x0, inc0], deg_b, *tables, False, t_blk)
    inc_b = exchange(side_b, HALF)
    cur, side = diffuse(a_sets, [cur_a, cur_b, inc_a, inc_b], deg_ab, *tables, False, t_blk)
    inc = exchange(side, BS)
    last, side = diffuse(a_sets, [cur, inc], deg_ab, *tables, True, t_blk)
    last = last.reshape(BLK_DEV * BS, genes)
    top_end = side[0]
    top_end = jnp.max(lax.all_gather(top_end, "cell"), axis=0)
    return last * (top_start / top_end)[None, :]


def solution(mesh):
    return jax.shard_map(
        on_device,
        mesh=mesh,
        in_specs=(P("cell", "gene"), P("cell", "gene", None), P("cell"), P("cell"), P("cell")),
        out_specs=P("cell", "gene"),
        check_vma=False,
    )
```

```python
import functools

import jax
import jax.numpy as jnp
from jax import lax
from jax.experimental import pallas as pl
from jax.experimental.pallas import tpu as pltpu
from jax.sharding import PartitionSpec as P

BS = 256
BLK_DEV = 32
REQ_CAP = 3
STEPS = 3
UNROLL = 25
HALF = BS // 2
CHUNK = 32


def ranks_of(owner, remote):
    count = owner.shape[-1]
    order = jnp.arange(count, dtype=jnp.int32)
    earlier = order[None, :] < order[:, None]
    same = (owner[..., :, None] == owner[..., None, :]) & remote[..., None, :] & earlier
    return jnp.sum(same.astype(jnp.int32), axis=-1)


def interleave(first, second):
    pieces = []
    for g in range(first.shape[0] // CHUNK):
        pieces.append(first[g * CHUNK:(g + 1) * CHUNK])
        pieces.append(second[g * CHUNK:(g + 1) * CHUNK])
    return jnp.concatenate(pieces, axis=0)


def step_kernel(n_a, split_x, final, t_blk, src_ref, row_ref, kind_ref, ask_ref, *refs):
    a_refs = refs[:n_a]
    refs = refs[n_a:]
    if split_x:
        cura_ref, curb_ref, inca_ref, incb_ref = refs[:4]
        refs = refs[4:]
    else:
        cur_ref, inc_ref = refs[:2]
        refs = refs[2:]
    deg_ref, out_ref, side_ref, acc_ref = refs
    s = pl.program_id(0)
    last = pl.num_programs(0) - 1

    @pl.when(s == 0)
    def _():
        acc_ref[...] = jnp.zeros_like(acc_ref)

    def body(j, carry):
        t = s * t_blk + j
        r = row_ref[t]
        c = src_ref[t]
        rem = kind_ref[t] == 3
        cl = jnp.minimum(c, BLK_DEV - 1)
        if split_x:
            xa = jnp.where(rem, inca_ref[c], cura_ref[cl])
            xb = jnp.where(rem, incb_ref[c], curb_ref[cl])
            x = interleave(xa, xb)
        else:
            x = jnp.where(rem, inc_ref[c], cur_ref[cl])
        for p in range(n_a):
            acc_ref[r, p * HALF:(p + 1) * HALF, :] += jnp.dot(a_refs[p][j], x, preferred_element_type=jnp.float32)
        return carry

    lax.fori_loop(0, t_blk, body, 0, unroll=UNROLL)

    @pl.when(s == last)
    def _():
        deg_cols = deg_ref[...].T
        m = jnp.full((1, out_ref.shape[-1]), -jnp.inf, jnp.float32)
        for r in range(BLK_DEV):
            val = acc_ref[r] / deg_cols[:, r:r + 1]
            if n_a == 2:
                val = interleave(val[:HALF], val[HALF:])
            out_ref[r] = val.astype(out_ref.dtype)
            if final:
                m = jnp.maximum(m, jnp.max(val, axis=0, keepdims=True))
        if final:
            side_ref[...] = jnp.broadcast_to(m, side_ref.shape)
        else:
            def send(q, carry):
                side_ref[q] = out_ref[ask_ref[q]]
                return carry

            lax.fori_loop(0, side_ref.shape[0], send, 0)


def diffuse(a_parts, xs, deg, src, rows, kind, asked, final, t_blk):
    slots = a_parts[0].shape[0]
    genes = xs[0].shape[-1]
    n_a = len(a_parts)
    split_x = len(xs) == 4
    n_ask = asked.shape[0]
    out_rows = HALF * n_a

    def full(shape):
        return pl.BlockSpec(shape, lambda s, *_: (0,) * len(shape), pipeline_mode=pl.Buffered(1))

    in_specs = [pl.BlockSpec((t_blk, HALF, BS), lambda s, *_: (s, 0, 0)) for _ in a_parts]
    in_specs += [full(x.shape) for x in xs]
    in_specs.append(full(deg.shape))
    out_block = pl.BlockSpec((BLK_DEV, out_rows, genes), lambda s, *_: (0, 0, 0))
    if final:
        out_specs = [out_block, pl.BlockSpec((8, genes), lambda s, *_: (0, 0))]
        out_shape = [
            jax.ShapeDtypeStruct((BLK_DEV, out_rows, genes), jnp.float32),
            jax.ShapeDtypeStruct((8, genes), jnp.float32),
        ]
    else:
        out_specs = [out_block, pl.BlockSpec((n_ask, out_rows, genes), lambda s, *_: (0, 0, 0))]
        out_shape = [
            jax.ShapeDtypeStruct((BLK_DEV, out_rows, genes), jnp.bfloat16),
            jax.ShapeDtypeStruct((n_ask, out_rows, genes), jnp.bfloat16),
        ]
    grid_spec = pltpu.PrefetchScalarGridSpec(
        num_scalar_prefetch=4,
        grid=(slots // t_blk,),
        in_specs=in_specs,
        out_specs=out_specs,
        scratch_shapes=[pltpu.VMEM((BLK_DEV + 1, out_rows, genes), jnp.float32)],
    )
    return pl.pallas_call(
        functools.partial(step_kernel, n_a, split_x, final, t_blk),
        grid_spec=grid_spec,
        out_shape=out_shape,
        compiler_params=pltpu.CompilerParams(
            dimension_semantics=("arbitrary",), vmem_limit_bytes=60 * 1024 * 1024
        ),
    )(src, rows, kind, asked, *a_parts, *xs, deg)


def on_device(expression, affinity, tile_rows, tile_cols, tile_count):
    me = lax.axis_index("cell")
    gi = lax.axis_index("gene")
    peers = lax.axis_size("cell")
    n_gene = lax.axis_size("gene")
    genes = expression.shape[1]
    part_rows = affinity.shape[1]
    slots = affinity.shape[0]
    order = jnp.arange(slots, dtype=jnp.int32)
    valid = order < tile_count[0]
    local_row = tile_rows - me * BLK_DEV
    row_index = jnp.clip(jnp.where(valid, local_row, 0), 0, BLK_DEV - 1)
    junk_row = jnp.where(valid, row_index, BLK_DEV).astype(jnp.int32)
    used = min(slots, BLK_DEV + (peers - 1) * REQ_CAP)
    t_blk = max(d for d in range(1, 33) if used % d == 0)
    owner = tile_cols // BLK_DEV
    col_slot = tile_cols - owner * BLK_DEV
    remote = valid & (owner != me)
    selfish = valid & (tile_rows == tile_cols)

    diag = (
        lax.broadcasted_iota(jnp.int32, (part_rows, BS), 0) + gi * part_rows
        == lax.broadcasted_iota(jnp.int32, (part_rows, BS), 1)
    )
    sub = part_rows // 2

    def set_part(h):
        d = diag[h * sub:(h + 1) * sub]
        keep = valid[:used, None, None] & jnp.logical_not(selfish[:used, None, None] & d[None])
        a = affinity[:used, h * sub:(h + 1) * sub]
        return jnp.where(keep, a, jnp.zeros_like(a))

    set_parts = [set_part(h) for h in range(2)]
    a_sets = [lax.all_gather(p, "gene", axis=1, tiled=True) for p in set_parts]
    aff_sums = lax.optimization_barrier(affinity[:used])
    keep_all = valid[:used, None, None] & jnp.logical_not(selfish[:used, None, None] & diag[None])
    part_sums = jnp.sum(jnp.where(keep_all, aff_sums, jnp.zeros_like(aff_sums)), axis=-1, dtype=jnp.float32)
    part_deg = jax.ops.segment_sum(part_sums, row_index[:used], BLK_DEV)
    deg = lax.all_gather(part_deg, "gene", axis=1, tiled=True)
    deg_sets = deg.reshape(BLK_DEV, n_gene, 2, sub)
    deg_a = deg_sets[:, :, 0].reshape(BLK_DEV, HALF)
    deg_b = deg_sets[:, :, 1].reshape(BLK_DEV, HALF)
    deg_ab = jnp.concatenate([deg_a, deg_b], axis=1)

    rank = ranks_of(owner, remote)
    peer_ids = jnp.arange(peers, dtype=jnp.int32)
    place = jnp.arange(REQ_CAP, dtype=jnp.int32)
    hit = (
        remote[:, None, None]
        & (owner[:, None, None] == peer_ids[None, :, None])
        & (rank[:, None, None] == place[None, None, :])
    )
    wanted = jnp.sum(jnp.where(hit, col_slot[:, None, None] + 1, 0), axis=0) - 1
    top_start = jnp.max(expression, axis=0).astype(jnp.float32)
    request = jnp.concatenate(
        [wanted.astype(jnp.float32), jnp.broadcast_to(top_start[None, :], (peers, genes))], axis=1
    )
    reply = lax.all_to_all(request, "cell", split_axis=0, concat_axis=0, tiled=True)
    asked = jnp.clip(reply[:, :REQ_CAP].astype(jnp.int32), 0, BLK_DEV - 1).reshape(-1)
    top_start = jnp.max(reply[:, REQ_CAP:], axis=0)

    kind = jnp.where(remote, 3, jnp.where(selfish, 2, jnp.where(valid, 1, 0))).astype(jnp.int32)
    src = jnp.where(remote, owner * REQ_CAP + rank, jnp.where(valid, col_slot, 0))
    src = jnp.where(remote, jnp.clip(src, 0, peers * REQ_CAP - 1), jnp.clip(src, 0, BLK_DEV - 1)).astype(jnp.int32)
    tables = (src, junk_row, kind, asked)

    def exchange(out, rows_):
        got = lax.all_to_all(
            out.reshape(peers, REQ_CAP, rows_, genes), "cell", split_axis=0, concat_axis=0, tiled=True
        )
        return got.reshape(peers * REQ_CAP, rows_, genes)

    x0 = expression.reshape(BLK_DEV, BS, genes)
    inc0 = exchange(x0[asked], BS)
    cur_a, side_a = diffuse([a_sets[0]], [x0, inc0], deg_a, *tables, False, t_blk)
    inc_a = exchange(side_a, HALF)
    cur_b, side_b = diffuse([a_sets[1]], [x0, inc0], deg_b, *tables, False, t_blk)
    inc_b = exchange(side_b, HALF)
    cur, side = diffuse(a_sets, [cur_a, cur_b, inc_a, inc_b], deg_ab, *tables, False, t_blk)
    inc = exchange(side, BS)
    last, side = diffuse(a_sets, [cur, inc], deg_ab, *tables, True, t_blk)
    last = last.reshape(BLK_DEV * BS, genes)
    top_end = side[0]
    top_end = jnp.max(
        lax.all_to_all(jnp.broadcast_to(top_end[None, :], (peers, genes)), "cell", 0, 0, tiled=True), axis=0
    )
    return last * (top_start / top_end)[None, :]


def solution(mesh):
    return jax.shard_map(
        on_device,
        mesh=mesh,
        in_specs=(P("cell", "gene"), P("cell", "gene", None), P("cell"), P("cell"), P("cell")),
        out_specs=P("cell", "gene"),
        check_vma=False,
    )
```

```python
import functools

import jax
import jax.numpy as jnp
from jax import lax
from jax.experimental import pallas as pl
from jax.experimental.pallas import tpu as pltpu
from jax.sharding import PartitionSpec as P

BS = 256
BLK_DEV = 32
REQ_CAP = 3
STEPS = 3
UNROLL = 25
HALF = BS // 2
CHUNK = 32


def ranks_of(owner, remote):
    count = owner.shape[-1]
    order = jnp.arange(count, dtype=jnp.int32)
    earlier = order[None, :] < order[:, None]
    same = (owner[..., :, None] == owner[..., None, :]) & remote[..., None, :] & earlier
    return jnp.sum(same.astype(jnp.int32), axis=-1)


def interleave(first, second):
    pieces = []
    for g in range(first.shape[0] // CHUNK):
        pieces.append(first[g * CHUNK:(g + 1) * CHUNK])
        pieces.append(second[g * CHUNK:(g + 1) * CHUNK])
    return jnp.concatenate(pieces, axis=0)


def step_kernel(n_a, split_x, final, t_blk, src_ref, row_ref, kind_ref, ask_ref, *refs):
    a_refs = refs[:n_a]
    refs = refs[n_a:]
    if split_x:
        cura_ref, curb_ref, inca_ref, incb_ref = refs[:4]
        refs = refs[4:]
    else:
        cur_ref, inc_ref = refs[:2]
        refs = refs[2:]
    deg_ref, out_ref, side_ref, acc_ref = refs
    s = pl.program_id(0)
    last = pl.num_programs(0) - 1

    @pl.when(s == 0)
    def _():
        acc_ref[...] = jnp.zeros_like(acc_ref)

    def body(j, carry):
        t = s * t_blk + j
        r = row_ref[t]
        c = src_ref[t]
        rem = kind_ref[t] == 3
        cl = jnp.minimum(c, BLK_DEV - 1)
        if split_x:
            xa = jnp.where(rem, inca_ref[c], cura_ref[cl])
            xb = jnp.where(rem, incb_ref[c], curb_ref[cl])
            x = interleave(xa, xb)
        else:
            x = jnp.where(rem, inc_ref[c], cur_ref[cl])
        for p in range(n_a):
            acc_ref[r, p * HALF:(p + 1) * HALF, :] += jnp.dot(a_refs[p][j], x, preferred_element_type=jnp.float32)
        return carry

    lax.fori_loop(0, t_blk, body, 0, unroll=UNROLL)

    @pl.when(s == last)
    def _():
        deg_cols = deg_ref[...].T
        m = jnp.full((1, out_ref.shape[-1]), -jnp.inf, jnp.float32)
        for r in range(BLK_DEV):
            val = acc_ref[r] / deg_cols[:, r:r + 1]
            if n_a == 2:
                val = interleave(val[:HALF], val[HALF:])
            out_ref[r] = val.astype(out_ref.dtype)
            if final:
                m = jnp.maximum(m, jnp.max(val, axis=0, keepdims=True))
        if final:
            side_ref[...] = jnp.broadcast_to(m, side_ref.shape)
        else:
            def send(q, carry):
                side_ref[q] = out_ref[ask_ref[q]]
                return carry

            lax.fori_loop(0, side_ref.shape[0], send, 0, unroll=8)


def diffuse(a_parts, xs, deg, src, rows, kind, asked, final, t_blk):
    slots = a_parts[0].shape[0]
    genes = xs[0].shape[-1]
    n_a = len(a_parts)
    split_x = len(xs) == 4
    n_ask = asked.shape[0]
    out_rows = HALF * n_a

    def full(shape):
        return pl.BlockSpec(shape, lambda s, *_: (0,) * len(shape), pipeline_mode=pl.Buffered(1))

    in_specs = [pl.BlockSpec((t_blk, HALF, BS), lambda s, *_: (s, 0, 0)) for _ in a_parts]
    in_specs += [full(x.shape) for x in xs]
    in_specs.append(full(deg.shape))
    out_block = pl.BlockSpec((BLK_DEV, out_rows, genes), lambda s, *_: (0, 0, 0))
    if final:
        out_specs = [out_block, pl.BlockSpec((8, genes), lambda s, *_: (0, 0))]
        out_shape = [
            jax.ShapeDtypeStruct((BLK_DEV, out_rows, genes), jnp.float32),
            jax.ShapeDtypeStruct((8, genes), jnp.float32),
        ]
    else:
        out_specs = [out_block, pl.BlockSpec((n_ask, out_rows, genes), lambda s, *_: (0, 0, 0))]
        out_shape = [
            jax.ShapeDtypeStruct((BLK_DEV, out_rows, genes), jnp.bfloat16),
            jax.ShapeDtypeStruct((n_ask, out_rows, genes), jnp.bfloat16),
        ]
    grid_spec = pltpu.PrefetchScalarGridSpec(
        num_scalar_prefetch=4,
        grid=(slots // t_blk,),
        in_specs=in_specs,
        out_specs=out_specs,
        scratch_shapes=[pltpu.VMEM((BLK_DEV + 1, out_rows, genes), jnp.float32)],
    )
    return pl.pallas_call(
        functools.partial(step_kernel, n_a, split_x, final, t_blk),
        grid_spec=grid_spec,
        out_shape=out_shape,
        compiler_params=pltpu.CompilerParams(
            dimension_semantics=("arbitrary",), vmem_limit_bytes=60 * 1024 * 1024
        ),
    )(src, rows, kind, asked, *a_parts, *xs, deg)


def on_device(expression, affinity, tile_rows, tile_cols, tile_count):
    me = lax.axis_index("cell")
    gi = lax.axis_index("gene")
    peers = lax.axis_size("cell")
    n_gene = lax.axis_size("gene")
    genes = expression.shape[1]
    part_rows = affinity.shape[1]
    slots = affinity.shape[0]
    order = jnp.arange(slots, dtype=jnp.int32)
    valid = order < tile_count[0]
    local_row = tile_rows - me * BLK_DEV
    row_index = jnp.clip(jnp.where(valid, local_row, 0), 0, BLK_DEV - 1)
    junk_row = jnp.where(valid, row_index, BLK_DEV).astype(jnp.int32)
    used = min(slots, BLK_DEV + (peers - 1) * REQ_CAP)
    t_blk = max(d for d in range(1, 33) if used % d == 0)
    owner = tile_cols // BLK_DEV
    col_slot = tile_cols - owner * BLK_DEV
    remote = valid & (owner != me)
    selfish = valid & (tile_rows == tile_cols)

    diag = (
        lax.broadcasted_iota(jnp.int32, (part_rows, BS), 0) + gi * part_rows
        == lax.broadcasted_iota(jnp.int32, (part_rows, BS), 1)
    )
    sub = part_rows // 2

    def set_part(h):
        d = diag[h * sub:(h + 1) * sub]
        keep = valid[:used, None, None] & jnp.logical_not(selfish[:used, None, None] & d[None])
        a = affinity[:used, h * sub:(h + 1) * sub]
        return jnp.where(keep, a, jnp.zeros_like(a))

    set_parts = [set_part(h) for h in range(2)]
    a_sets = [lax.all_gather(p, "gene", axis=1, tiled=True) for p in set_parts]
    aff_sums = lax.optimization_barrier(affinity[:used])
    keep_all = valid[:used, None, None] & jnp.logical_not(selfish[:used, None, None] & diag[None])
    part_sums = jnp.sum(jnp.where(keep_all, aff_sums, jnp.zeros_like(aff_sums)), axis=-1, dtype=jnp.float32)
    part_deg = jax.ops.segment_sum(part_sums, row_index[:used], BLK_DEV)
    deg = lax.all_gather(part_deg, "gene", axis=1, tiled=True)
    deg_sets = deg.reshape(BLK_DEV, n_gene, 2, sub)
    deg_a = deg_sets[:, :, 0].reshape(BLK_DEV, HALF)
    deg_b = deg_sets[:, :, 1].reshape(BLK_DEV, HALF)
    deg_ab = jnp.concatenate([deg_a, deg_b], axis=1)

    rank = ranks_of(owner, remote)
    peer_ids = jnp.arange(peers, dtype=jnp.int32)
    place = jnp.arange(REQ_CAP, dtype=jnp.int32)
    hit = (
        remote[:, None, None]
        & (owner[:, None, None] == peer_ids[None, :, None])
        & (rank[:, None, None] == place[None, None, :])
    )
    wanted = jnp.sum(jnp.where(hit, col_slot[:, None, None] + 1, 0), axis=0) - 1
    top_start = jnp.max(expression, axis=0).astype(jnp.float32)
    request = jnp.concatenate(
        [wanted.astype(jnp.float32), jnp.broadcast_to(top_start[None, :], (peers, genes))], axis=1
    )
    reply = lax.all_to_all(request, "cell", split_axis=0, concat_axis=0, tiled=True)
    asked = jnp.clip(reply[:, :REQ_CAP].astype(jnp.int32), 0, BLK_DEV - 1).reshape(-1)
    top_start = jnp.max(reply[:, REQ_CAP:], axis=0)

    kind = jnp.where(remote, 3, jnp.where(selfish, 2, jnp.where(valid, 1, 0))).astype(jnp.int32)
    src = jnp.where(remote, owner * REQ_CAP + rank, jnp.where(valid, col_slot, 0))
    src = jnp.where(remote, jnp.clip(src, 0, peers * REQ_CAP - 1), jnp.clip(src, 0, BLK_DEV - 1)).astype(jnp.int32)
    tables = (src, junk_row, kind, asked)

    def exchange(out, rows_):
        got = lax.all_to_all(
            out.reshape(peers, REQ_CAP, rows_, genes), "cell", split_axis=0, concat_axis=0, tiled=True
        )
        return got.reshape(peers * REQ_CAP, rows_, genes)

    x0 = expression.reshape(BLK_DEV, BS, genes)
    inc0 = exchange(x0[asked], BS)
    cur_a, side_a = diffuse([a_sets[0]], [x0, inc0], deg_a, *tables, False, t_blk)
    inc_a = exchange(side_a, HALF)
    cur_b, side_b = diffuse([a_sets[1]], [x0, inc0], deg_b, *tables, False, t_blk)
    inc_b = exchange(side_b, HALF)
    cur, side = diffuse(a_sets, [cur_a, cur_b, inc_a, inc_b], deg_ab, *tables, False, t_blk)
    inc = exchange(side, BS)
    last, side = diffuse(a_sets, [cur, inc], deg_ab, *tables, True, t_blk)
    last = last.reshape(BLK_DEV * BS, genes)
    top_end = side[0]
    top_end = jnp.max(
        lax.all_to_all(jnp.broadcast_to(top_end[None, :], (peers, genes)), "cell", 0, 0, tiled=True), axis=0
    )
    return last * (top_start / top_end)[None, :]


def solution(mesh):
    return jax.shard_map(
        on_device,
        mesh=mesh,
        in_specs=(P("cell", "gene"), P("cell", "gene", None), P("cell"), P("cell"), P("cell")),
        out_specs=P("cell", "gene"),
        check_vma=False,
    )
```

```python
import functools

import jax
import jax.numpy as jnp
from jax import lax
from jax.experimental import pallas as pl
from jax.experimental.pallas import tpu as pltpu
from jax.sharding import PartitionSpec as P

BS = 256
BLK_DEV = 32
REQ_CAP = 3
STEPS = 3
UNROLL = 25
HALF = BS // 2
CHUNK = 32


def ranks_of(owner, remote):
    count = owner.shape[-1]
    order = jnp.arange(count, dtype=jnp.int32)
    earlier = order[None, :] < order[:, None]
    same = (owner[..., :, None] == owner[..., None, :]) & remote[..., None, :] & earlier
    return jnp.sum(same.astype(jnp.int32), axis=-1)


def interleave(first, second):
    pieces = []
    for g in range(first.shape[0] // CHUNK):
        pieces.append(first[g * CHUNK:(g + 1) * CHUNK])
        pieces.append(second[g * CHUNK:(g + 1) * CHUNK])
    return jnp.concatenate(pieces, axis=0)


def step_kernel(n_a, split_x, final, t_blk, src_ref, row_ref, kind_ref, ask_ref, *refs):
    a_refs = refs[:n_a]
    refs = refs[n_a:]
    if split_x:
        cura_ref, curb_ref, inca_ref, incb_ref = refs[:4]
        refs = refs[4:]
    else:
        cur_ref, inc_ref = refs[:2]
        refs = refs[2:]
    deg_ref, out_ref, side_ref, acc_ref = refs[:4]
    s = pl.program_id(0)
    last = pl.num_programs(0) - 1

    @pl.when(s == 0)
    def _():
        acc_ref[...] = jnp.zeros_like(acc_ref)

    def body(j, carry):
        t = s * t_blk + j
        r = row_ref[t]
        c = src_ref[t]
        rem = kind_ref[t] == 3
        cl = jnp.minimum(c, BLK_DEV - 1)
        if split_x:
            xa = jnp.where(rem, inca_ref[c], cura_ref[cl])
            xb = jnp.where(rem, incb_ref[c], curb_ref[cl])
            x = interleave(xa, xb)
        else:
            x = jnp.where(rem, inc_ref[c], cur_ref[cl])
        for p in range(n_a):
            acc_ref[r, p * HALF:(p + 1) * HALF, :] += jnp.dot(a_refs[p][j], x, preferred_element_type=jnp.float32)
        return carry

    lax.fori_loop(0, t_blk, body, 0, unroll=UNROLL)

    @pl.when(s == last)
    def _():
        deg_cols = deg_ref[...].T
        m = jnp.full((1, out_ref.shape[-1]), -jnp.inf, jnp.float32)
        for r in range(BLK_DEV):
            val = acc_ref[r] / deg_cols[:, r:r + 1]
            if n_a == 2:
                val = interleave(val[:HALF], val[HALF:])
            out_ref[r] = val.astype(out_ref.dtype)
            if final:
                m = jnp.maximum(m, jnp.max(val, axis=0, keepdims=True))
        if final:
            side_ref[...] = jnp.broadcast_to(m, side_ref.shape)
        else:
            sems = refs[4]
            n_send = side_ref.shape[0]

            def send(q, carry):
                pltpu.make_async_copy(out_ref.at[ask_ref[q]], side_ref.at[q], sems.at[q]).start()
                return carry

            def landed(q, carry):
                pltpu.make_async_copy(out_ref.at[0], side_ref.at[q], sems.at[q]).wait()
                return carry

            lax.fori_loop(0, n_send, send, 0, unroll=8)
            lax.fori_loop(0, n_send, landed, 0, unroll=8)


def diffuse(a_parts, xs, deg, src, rows, kind, asked, final, t_blk):
    slots = a_parts[0].shape[0]
    genes = xs[0].shape[-1]
    n_a = len(a_parts)
    split_x = len(xs) == 4
    n_ask = asked.shape[0]
    out_rows = HALF * n_a

    def full(shape):
        return pl.BlockSpec(shape, lambda s, *_: (0,) * len(shape), pipeline_mode=pl.Buffered(1))

    in_specs = [pl.BlockSpec((t_blk, HALF, BS), lambda s, *_: (s, 0, 0)) for _ in a_parts]
    in_specs += [full(x.shape) for x in xs]
    in_specs.append(full(deg.shape))
    out_block = pl.BlockSpec((BLK_DEV, out_rows, genes), lambda s, *_: (0, 0, 0))
    if final:
        out_specs = [out_block, pl.BlockSpec((8, genes), lambda s, *_: (0, 0))]
        out_shape = [
            jax.ShapeDtypeStruct((BLK_DEV, out_rows, genes), jnp.float32),
            jax.ShapeDtypeStruct((8, genes), jnp.float32),
        ]
    else:
        out_specs = [out_block, pl.BlockSpec(memory_space=pl.ANY)]
        out_shape = [
            jax.ShapeDtypeStruct((BLK_DEV, out_rows, genes), jnp.bfloat16),
            jax.ShapeDtypeStruct((n_ask, out_rows, genes), jnp.bfloat16),
        ]
    grid_spec = pltpu.PrefetchScalarGridSpec(
        num_scalar_prefetch=4,
        grid=(slots // t_blk,),
        in_specs=in_specs,
        out_specs=out_specs,
        scratch_shapes=[pltpu.VMEM((BLK_DEV + 1, out_rows, genes), jnp.float32)]
        + ([] if final else [pltpu.SemaphoreType.DMA((n_ask,))]),
    )
    return pl.pallas_call(
        functools.partial(step_kernel, n_a, split_x, final, t_blk),
        grid_spec=grid_spec,
        out_shape=out_shape,
        compiler_params=pltpu.CompilerParams(
            dimension_semantics=("arbitrary",), vmem_limit_bytes=60 * 1024 * 1024
        ),
    )(src, rows, kind, asked, *a_parts, *xs, deg)


def on_device(expression, affinity, tile_rows, tile_cols, tile_count):
    me = lax.axis_index("cell")
    gi = lax.axis_index("gene")
    peers = lax.axis_size("cell")
    n_gene = lax.axis_size("gene")
    genes = expression.shape[1]
    part_rows = affinity.shape[1]
    slots = affinity.shape[0]
    order = jnp.arange(slots, dtype=jnp.int32)
    valid = order < tile_count[0]
    local_row = tile_rows - me * BLK_DEV
    row_index = jnp.clip(jnp.where(valid, local_row, 0), 0, BLK_DEV - 1)
    junk_row = jnp.where(valid, row_index, BLK_DEV).astype(jnp.int32)
    used = min(slots, BLK_DEV + (peers - 1) * REQ_CAP)
    t_blk = max(d for d in range(1, 33) if used % d == 0)
    owner = tile_cols // BLK_DEV
    col_slot = tile_cols - owner * BLK_DEV
    remote = valid & (owner != me)
    selfish = valid & (tile_rows == tile_cols)

    diag = (
        lax.broadcasted_iota(jnp.int32, (part_rows, BS), 0) + gi * part_rows
        == lax.broadcasted_iota(jnp.int32, (part_rows, BS), 1)
    )
    sub = part_rows // 2

    def set_part(h):
        d = diag[h * sub:(h + 1) * sub]
        keep = valid[:used, None, None] & jnp.logical_not(selfish[:used, None, None] & d[None])
        a = affinity[:used, h * sub:(h + 1) * sub]
        return jnp.where(keep, a, jnp.zeros_like(a))

    set_parts = [set_part(h) for h in range(2)]
    a_sets = [lax.all_gather(p, "gene", axis=1, tiled=True) for p in set_parts]
    aff_sums = lax.optimization_barrier(affinity[:used])
    keep_all = valid[:used, None, None] & jnp.logical_not(selfish[:used, None, None] & diag[None])
    part_sums = jnp.sum(jnp.where(keep_all, aff_sums, jnp.zeros_like(aff_sums)), axis=-1, dtype=jnp.float32)
    part_deg = jax.ops.segment_sum(part_sums, row_index[:used], BLK_DEV)
    deg = lax.all_gather(part_deg, "gene", axis=1, tiled=True)
    deg_sets = deg.reshape(BLK_DEV, n_gene, 2, sub)
    deg_a = deg_sets[:, :, 0].reshape(BLK_DEV, HALF)
    deg_b = deg_sets[:, :, 1].reshape(BLK_DEV, HALF)
    deg_ab = jnp.concatenate([deg_a, deg_b], axis=1)

    rank = ranks_of(owner, remote)
    peer_ids = jnp.arange(peers, dtype=jnp.int32)
    place = jnp.arange(REQ_CAP, dtype=jnp.int32)
    hit = (
        remote[:, None, None]
        & (owner[:, None, None] == peer_ids[None, :, None])
        & (rank[:, None, None] == place[None, None, :])
    )
    wanted = jnp.sum(jnp.where(hit, col_slot[:, None, None] + 1, 0), axis=0) - 1
    top_start = jnp.max(expression, axis=0).astype(jnp.float32)
    request = jnp.concatenate(
        [wanted.astype(jnp.float32), jnp.broadcast_to(top_start[None, :], (peers, genes))], axis=1
    )
    reply = lax.all_to_all(request, "cell", split_axis=0, concat_axis=0, tiled=True)
    asked = jnp.clip(reply[:, :REQ_CAP].astype(jnp.int32), 0, BLK_DEV - 1).reshape(-1)
    top_start = jnp.max(reply[:, REQ_CAP:], axis=0)

    kind = jnp.where(remote, 3, jnp.where(selfish, 2, jnp.where(valid, 1, 0))).astype(jnp.int32)
    src = jnp.where(remote, owner * REQ_CAP + rank, jnp.where(valid, col_slot, 0))
    src = jnp.where(remote, jnp.clip(src, 0, peers * REQ_CAP - 1), jnp.clip(src, 0, BLK_DEV - 1)).astype(jnp.int32)
    tables = (src, junk_row, kind, asked)

    def exchange(out, rows_):
        got = lax.all_to_all(
            out.reshape(peers, REQ_CAP, rows_, genes), "cell", split_axis=0, concat_axis=0, tiled=True
        )
        return got.reshape(peers * REQ_CAP, rows_, genes)

    x0 = expression.reshape(BLK_DEV, BS, genes)
    inc0 = exchange(x0[asked], BS)
    cur_a, side_a = diffuse([a_sets[0]], [x0, inc0], deg_a, *tables, False, t_blk)
    inc_a = exchange(side_a, HALF)
    cur_b, side_b = diffuse([a_sets[1]], [x0, inc0], deg_b, *tables, False, t_blk)
    inc_b = exchange(side_b, HALF)
    cur, side = diffuse(a_sets, [cur_a, cur_b, inc_a, inc_b], deg_ab, *tables, False, t_blk)
    inc = exchange(side, BS)
    last, side = diffuse(a_sets, [cur, inc], deg_ab, *tables, True, t_blk)
    last = last.reshape(BLK_DEV * BS, genes)
    top_end = side[0]
    top_end = jnp.max(
        lax.all_to_all(jnp.broadcast_to(top_end[None, :], (peers, genes)), "cell", 0, 0, tiled=True), axis=0
    )
    return last * (top_start / top_end)[None, :]


def solution(mesh):
    return jax.shard_map(
        on_device,
        mesh=mesh,
        in_specs=(P("cell", "gene"), P("cell", "gene", None), P("cell"), P("cell"), P("cell")),
        out_specs=P("cell", "gene"),
        check_vma=False,
    )
```

```python
import functools

import jax
import jax.numpy as jnp
from jax import lax
from jax.experimental import pallas as pl
from jax.experimental.pallas import tpu as pltpu
from jax.sharding import PartitionSpec as P

BS = 256
BLK_DEV = 32
REQ_CAP = 3
STEPS = 3
UNROLL = 25
HALF = BS // 2
CHUNK = 32


def ranks_of(owner, remote):
    count = owner.shape[-1]
    order = jnp.arange(count, dtype=jnp.int32)
    earlier = order[None, :] < order[:, None]
    same = (owner[..., :, None] == owner[..., None, :]) & remote[..., None, :] & earlier
    return jnp.sum(same.astype(jnp.int32), axis=-1)


def interleave(first, second):
    pieces = []
    for g in range(first.shape[0] // CHUNK):
        pieces.append(first[g * CHUNK:(g + 1) * CHUNK])
        pieces.append(second[g * CHUNK:(g + 1) * CHUNK])
    return jnp.concatenate(pieces, axis=0)


def step_kernel(n_a, split_x, final, t_blk, src_ref, row_ref, kind_ref, ask_ref, *refs):
    a_refs = refs[:n_a]
    refs = refs[n_a:]
    if split_x:
        cura_ref, curb_ref, inca_ref, incb_ref = refs[:4]
        refs = refs[4:]
    else:
        cur_ref, inc_ref = refs[:2]
        refs = refs[2:]
    deg_ref, out_ref, side_ref, acc_ref = refs
    s = pl.program_id(0)
    last = pl.num_programs(0) - 1

    @pl.when(s == 0)
    def _():
        acc_ref[...] = jnp.zeros_like(acc_ref)

    def body(j, carry):
        t = s * t_blk + j
        r = row_ref[t]
        c = src_ref[t]
        rem = kind_ref[t] == 3
        cl = jnp.minimum(c, BLK_DEV - 1)
        if split_x:
            xa = jnp.where(rem, inca_ref[c], cura_ref[cl])
            xb = jnp.where(rem, incb_ref[c], curb_ref[cl])
            x = interleave(xa, xb)
        else:
            x = jnp.where(rem, inc_ref[c], cur_ref[cl])
        for p in range(n_a):
            acc_ref[r, p * HALF:(p + 1) * HALF, :] += jnp.dot(a_refs[p][j], x, preferred_element_type=jnp.float32)
        return carry

    lax.fori_loop(0, t_blk, body, 0, unroll=UNROLL)

    @pl.when(s == last)
    def _():
        inv_cols = 1.0 / deg_ref[...].T
        m = jnp.full((1, out_ref.shape[-1]), -jnp.inf, jnp.float32)
        for r in range(BLK_DEV):
            val = acc_ref[r] * inv_cols[:, r:r + 1]
            if n_a == 2:
                val = interleave(val[:HALF], val[HALF:])
            out_ref[r] = val.astype(out_ref.dtype)
            if final:
                m = jnp.maximum(m, jnp.max(val, axis=0, keepdims=True))
        if final:
            side_ref[...] = jnp.broadcast_to(m, side_ref.shape)
        else:
            def send(q, carry):
                side_ref[q] = out_ref[ask_ref[q]]
                return carry

            lax.fori_loop(0, side_ref.shape[0], send, 0, unroll=8)


def diffuse(a_parts, xs, deg, src, rows, kind, asked, final, t_blk):
    slots = a_parts[0].shape[0]
    genes = xs[0].shape[-1]
    n_a = len(a_parts)
    split_x = len(xs) == 4
    n_ask = asked.shape[0]
    out_rows = HALF * n_a

    def full(shape):
        return pl.BlockSpec(shape, lambda s, *_: (0,) * len(shape), pipeline_mode=pl.Buffered(1))

    in_specs = [pl.BlockSpec((t_blk, HALF, BS), lambda s, *_: (s, 0, 0)) for _ in a_parts]
    in_specs += [full(x.shape) for x in xs]
    in_specs.append(full(deg.shape))
    out_block = pl.BlockSpec((BLK_DEV, out_rows, genes), lambda s, *_: (0, 0, 0))
    if final:
        out_specs = [out_block, pl.BlockSpec((8, genes), lambda s, *_: (0, 0))]
        out_shape = [
            jax.ShapeDtypeStruct((BLK_DEV, out_rows, genes), jnp.float32),
            jax.ShapeDtypeStruct((8, genes), jnp.float32),
        ]
    else:
        out_specs = [out_block, pl.BlockSpec((n_ask, out_rows, genes), lambda s, *_: (0, 0, 0))]
        out_shape = [
            jax.ShapeDtypeStruct((BLK_DEV, out_rows, genes), jnp.bfloat16),
            jax.ShapeDtypeStruct((n_ask, out_rows, genes), jnp.bfloat16),
        ]
    grid_spec = pltpu.PrefetchScalarGridSpec(
        num_scalar_prefetch=4,
        grid=(slots // t_blk,),
        in_specs=in_specs,
        out_specs=out_specs,
        scratch_shapes=[pltpu.VMEM((BLK_DEV + 1, out_rows, genes), jnp.float32)],
    )
    return pl.pallas_call(
        functools.partial(step_kernel, n_a, split_x, final, t_blk),
        grid_spec=grid_spec,
        out_shape=out_shape,
        compiler_params=pltpu.CompilerParams(
            dimension_semantics=("arbitrary",), vmem_limit_bytes=60 * 1024 * 1024
        ),
    )(src, rows, kind, asked, *a_parts, *xs, deg)


def on_device(expression, affinity, tile_rows, tile_cols, tile_count):
    me = lax.axis_index("cell")
    gi = lax.axis_index("gene")
    peers = lax.axis_size("cell")
    n_gene = lax.axis_size("gene")
    genes = expression.shape[1]
    part_rows = affinity.shape[1]
    slots = affinity.shape[0]
    order = jnp.arange(slots, dtype=jnp.int32)
    valid = order < tile_count[0]
    local_row = tile_rows - me * BLK_DEV
    row_index = jnp.clip(jnp.where(valid, local_row, 0), 0, BLK_DEV - 1)
    junk_row = jnp.where(valid, row_index, BLK_DEV).astype(jnp.int32)
    used = min(slots, BLK_DEV + (peers - 1) * REQ_CAP)
    t_blk = max(d for d in range(1, 33) if used % d == 0)
    owner = tile_cols // BLK_DEV
    col_slot = tile_cols - owner * BLK_DEV
    remote = valid & (owner != me)
    selfish = valid & (tile_rows == tile_cols)

    diag = (
        lax.broadcasted_iota(jnp.int32, (part_rows, BS), 0) + gi * part_rows
        == lax.broadcasted_iota(jnp.int32, (part_rows, BS), 1)
    )
    sub = part_rows // 2

    def set_part(h):
        d = diag[h * sub:(h + 1) * sub]
        keep = valid[:used, None, None] & jnp.logical_not(selfish[:used, None, None] & d[None])
        a = affinity[:used, h * sub:(h + 1) * sub]
        return jnp.where(keep, a, jnp.zeros_like(a))

    set_parts = [set_part(h) for h in range(2)]
    a_sets = [lax.all_gather(p, "gene", axis=1, tiled=True) for p in set_parts]
    aff_sums = lax.optimization_barrier(affinity[:used])
    keep_all = valid[:used, None, None] & jnp.logical_not(selfish[:used, None, None] & diag[None])
    part_sums = jnp.sum(jnp.where(keep_all, aff_sums, jnp.zeros_like(aff_sums)), axis=-1, dtype=jnp.float32)
    part_deg = jax.ops.segment_sum(part_sums, row_index[:used], BLK_DEV)
    deg = lax.all_gather(part_deg, "gene", axis=1, tiled=True)
    deg_sets = deg.reshape(BLK_DEV, n_gene, 2, sub)
    deg_a = deg_sets[:, :, 0].reshape(BLK_DEV, HALF)
    deg_b = deg_sets[:, :, 1].reshape(BLK_DEV, HALF)
    deg_ab = jnp.concatenate([deg_a, deg_b], axis=1)

    rank = ranks_of(owner, remote)
    peer_ids = jnp.arange(peers, dtype=jnp.int32)
    place = jnp.arange(REQ_CAP, dtype=jnp.int32)
    hit = (
        remote[:, None, None]
        & (owner[:, None, None] == peer_ids[None, :, None])
        & (rank[:, None, None] == place[None, None, :])
    )
    wanted = jnp.sum(jnp.where(hit, col_slot[:, None, None] + 1, 0), axis=0) - 1
    top_start = jnp.max(expression, axis=0).astype(jnp.float32)
    request = jnp.concatenate(
        [wanted.astype(jnp.float32), jnp.broadcast_to(top_start[None, :], (peers, genes))], axis=1
    )
    reply = lax.all_to_all(request, "cell", split_axis=0, concat_axis=0, tiled=True)
    asked = jnp.clip(reply[:, :REQ_CAP].astype(jnp.int32), 0, BLK_DEV - 1).reshape(-1)
    top_start = jnp.max(reply[:, REQ_CAP:], axis=0)

    kind = jnp.where(remote, 3, jnp.where(selfish, 2, jnp.where(valid, 1, 0))).astype(jnp.int32)
    src = jnp.where(remote, owner * REQ_CAP + rank, jnp.where(valid, col_slot, 0))
    src = jnp.where(remote, jnp.clip(src, 0, peers * REQ_CAP - 1), jnp.clip(src, 0, BLK_DEV - 1)).astype(jnp.int32)
    tables = (src, junk_row, kind, asked)

    def exchange(out, rows_):
        got = lax.all_to_all(
            out.reshape(peers, REQ_CAP, rows_, genes), "cell", split_axis=0, concat_axis=0, tiled=True
        )
        return got.reshape(peers * REQ_CAP, rows_, genes)

    x0 = expression.reshape(BLK_DEV, BS, genes)
    inc0 = exchange(x0[asked], BS)
    cur_a, side_a = diffuse([a_sets[0]], [x0, inc0], deg_a, *tables, False, t_blk)
    inc_a = exchange(side_a, HALF)
    cur_b, side_b = diffuse([a_sets[1]], [x0, inc0], deg_b, *tables, False, t_blk)
    inc_b = exchange(side_b, HALF)
    cur, side = diffuse(a_sets, [cur_a, cur_b, inc_a, inc_b], deg_ab, *tables, False, t_blk)
    inc = exchange(side, BS)
    last, side = diffuse(a_sets, [cur, inc], deg_ab, *tables, True, t_blk)
    last = last.reshape(BLK_DEV * BS, genes)
    top_end = side[0]
    top_end = jnp.max(
        lax.all_to_all(jnp.broadcast_to(top_end[None, :], (peers, genes)), "cell", 0, 0, tiled=True), axis=0
    )
    return last * (top_start / top_end)[None, :]


def solution(mesh):
    return jax.shard_map(
        on_device,
        mesh=mesh,
        in_specs=(P("cell", "gene"), P("cell", "gene", None), P("cell"), P("cell"), P("cell")),
        out_specs=P("cell", "gene"),
        check_vma=False,
    )
```

```python
import functools

import jax
import jax.numpy as jnp
from jax import lax
from jax.experimental import pallas as pl
from jax.experimental.pallas import tpu as pltpu
from jax.sharding import PartitionSpec as P

BS = 256
BLK_DEV = 32
REQ_CAP = 3
STEPS = 3
UNROLL = 25
HALF = BS // 2
CHUNK = 32


def ranks_of(owner, remote):
    count = owner.shape[-1]
    order = jnp.arange(count, dtype=jnp.int32)
    earlier = order[None, :] < order[:, None]
    same = (owner[..., :, None] == owner[..., None, :]) & remote[..., None, :] & earlier
    return jnp.sum(same.astype(jnp.int32), axis=-1)


def interleave(first, second):
    pieces = []
    for g in range(first.shape[0] // CHUNK):
        pieces.append(first[g * CHUNK:(g + 1) * CHUNK])
        pieces.append(second[g * CHUNK:(g + 1) * CHUNK])
    return jnp.concatenate(pieces, axis=0)


def step_kernel(n_a, split_x, final, t_blk, src_ref, row_ref, kind_ref, ask_ref, *refs):
    a_refs = refs[:n_a]
    refs = refs[n_a:]
    if split_x:
        cura_ref, curb_ref, inca_ref, incb_ref = refs[:4]
        refs = refs[4:]
    else:
        cur_ref, inc_ref = refs[:2]
        refs = refs[2:]
    deg_ref, out_ref, side_ref, acc_ref = refs
    s = pl.program_id(0)
    last = pl.num_programs(0) - 1

    @pl.when(s == 0)
    def _():
        acc_ref[...] = jnp.zeros_like(acc_ref)

    def body(j, carry):
        t = s * t_blk + j
        r = row_ref[t]
        c = src_ref[t]
        rem = kind_ref[t] == 3
        cl = jnp.minimum(c, BLK_DEV - 1)
        if split_x:
            xa = jnp.where(rem, inca_ref[c], cura_ref[cl])
            xb = jnp.where(rem, incb_ref[c], curb_ref[cl])
            x = interleave(xa, xb)
        else:
            x = jnp.where(rem, inc_ref[c], cur_ref[cl])
        for p in range(n_a):
            acc_ref[r, p * HALF:(p + 1) * HALF, :] += jnp.dot(a_refs[p][j], x, preferred_element_type=jnp.float32)
        return carry

    lax.fori_loop(0, t_blk, body, 0, unroll=UNROLL)

    @pl.when(s == last)
    def _():
        deg_cols = deg_ref[...].T
        m = jnp.full((1, out_ref.shape[-1]), -jnp.inf, jnp.float32)
        for r in range(BLK_DEV):
            val = acc_ref[r] / deg_cols[:, r:r + 1]
            if n_a == 2:
                val = interleave(val[:HALF], val[HALF:])
            out_ref[r] = val.astype(out_ref.dtype)
            if final:
                m = jnp.maximum(m, jnp.max(val, axis=0, keepdims=True))
        if final:
            side_ref[...] = jnp.broadcast_to(m, side_ref.shape)
        else:
            def send(q, carry):
                side_ref[q] = out_ref[ask_ref[q]]
                return carry

            lax.fori_loop(0, side_ref.shape[0], send, 0, unroll=True)


def diffuse(a_parts, xs, deg, src, rows, kind, asked, final, t_blk):
    slots = a_parts[0].shape[0]
    genes = xs[0].shape[-1]
    n_a = len(a_parts)
    split_x = len(xs) == 4
    n_ask = asked.shape[0]
    out_rows = HALF * n_a

    def full(shape):
        return pl.BlockSpec(shape, lambda s, *_: (0,) * len(shape), pipeline_mode=pl.Buffered(1))

    in_specs = [pl.BlockSpec((t_blk, HALF, BS), lambda s, *_: (s, 0, 0)) for _ in a_parts]
    in_specs += [full(x.shape) for x in xs]
    in_specs.append(full(deg.shape))
    out_block = pl.BlockSpec((BLK_DEV, out_rows, genes), lambda s, *_: (0, 0, 0))
    if final:
        out_specs = [out_block, pl.BlockSpec((8, genes), lambda s, *_: (0, 0))]
        out_shape = [
            jax.ShapeDtypeStruct((BLK_DEV, out_rows, genes), jnp.float32),
            jax.ShapeDtypeStruct((8, genes), jnp.float32),
        ]
    else:
        out_specs = [out_block, pl.BlockSpec((n_ask, out_rows, genes), lambda s, *_: (0, 0, 0))]
        out_shape = [
            jax.ShapeDtypeStruct((BLK_DEV, out_rows, genes), jnp.bfloat16),
            jax.ShapeDtypeStruct((n_ask, out_rows, genes), jnp.bfloat16),
        ]
    grid_spec = pltpu.PrefetchScalarGridSpec(
        num_scalar_prefetch=4,
        grid=(slots // t_blk,),
        in_specs=in_specs,
        out_specs=out_specs,
        scratch_shapes=[pltpu.VMEM((BLK_DEV + 1, out_rows, genes), jnp.float32)],
    )
    return pl.pallas_call(
        functools.partial(step_kernel, n_a, split_x, final, t_blk),
        grid_spec=grid_spec,
        out_shape=out_shape,
        compiler_params=pltpu.CompilerParams(
            dimension_semantics=("arbitrary",), vmem_limit_bytes=60 * 1024 * 1024
        ),
    )(src, rows, kind, asked, *a_parts, *xs, deg)


def on_device(expression, affinity, tile_rows, tile_cols, tile_count):
    me = lax.axis_index("cell")
    gi = lax.axis_index("gene")
    peers = lax.axis_size("cell")
    n_gene = lax.axis_size("gene")
    genes = expression.shape[1]
    part_rows = affinity.shape[1]
    slots = affinity.shape[0]
    order = jnp.arange(slots, dtype=jnp.int32)
    valid = order < tile_count[0]
    local_row = tile_rows - me * BLK_DEV
    row_index = jnp.clip(jnp.where(valid, local_row, 0), 0, BLK_DEV - 1)
    junk_row = jnp.where(valid, row_index, BLK_DEV).astype(jnp.int32)
    used = min(slots, BLK_DEV + (peers - 1) * REQ_CAP)
    t_blk = max(d for d in range(1, 33) if used % d == 0)
    owner = tile_cols // BLK_DEV
    col_slot = tile_cols - owner * BLK_DEV
    remote = valid & (owner != me)
    selfish = valid & (tile_rows == tile_cols)

    diag = (
        lax.broadcasted_iota(jnp.int32, (part_rows, BS), 0) + gi * part_rows
        == lax.broadcasted_iota(jnp.int32, (part_rows, BS), 1)
    )
    sub = part_rows // 2

    def set_part(h):
        d = diag[h * sub:(h + 1) * sub]
        keep = valid[:used, None, None] & jnp.logical_not(selfish[:used, None, None] & d[None])
        a = affinity[:used, h * sub:(h + 1) * sub]
        return jnp.where(keep, a, jnp.zeros_like(a))

    set_parts = [set_part(h) for h in range(2)]
    a_sets = [lax.all_gather(p, "gene", axis=1, tiled=True) for p in set_parts]
    aff_sums = lax.optimization_barrier(affinity[:used])
    keep_all = valid[:used, None, None] & jnp.logical_not(selfish[:used, None, None] & diag[None])
    part_sums = jnp.sum(jnp.where(keep_all, aff_sums, jnp.zeros_like(aff_sums)), axis=-1, dtype=jnp.float32)
    part_deg = jax.ops.segment_sum(part_sums, row_index[:used], BLK_DEV)
    deg = lax.all_gather(part_deg, "gene", axis=1, tiled=True)
    deg_sets = deg.reshape(BLK_DEV, n_gene, 2, sub)
    deg_a = deg_sets[:, :, 0].reshape(BLK_DEV, HALF)
    deg_b = deg_sets[:, :, 1].reshape(BLK_DEV, HALF)
    deg_ab = jnp.concatenate([deg_a, deg_b], axis=1)

    rank = ranks_of(owner, remote)
    peer_ids = jnp.arange(peers, dtype=jnp.int32)
    place = jnp.arange(REQ_CAP, dtype=jnp.int32)
    hit = (
        remote[:, None, None]
        & (owner[:, None, None] == peer_ids[None, :, None])
        & (rank[:, None, None] == place[None, None, :])
    )
    wanted = jnp.sum(jnp.where(hit, col_slot[:, None, None] + 1, 0), axis=0) - 1
    top_start = jnp.max(expression, axis=0).astype(jnp.float32)
    request = jnp.concatenate(
        [wanted.astype(jnp.float32), jnp.broadcast_to(top_start[None, :], (peers, genes))], axis=1
    )
    reply = lax.all_to_all(request, "cell", split_axis=0, concat_axis=0, tiled=True)
    asked = jnp.clip(reply[:, :REQ_CAP].astype(jnp.int32), 0, BLK_DEV - 1).reshape(-1)
    top_start = jnp.max(reply[:, REQ_CAP:], axis=0)

    kind = jnp.where(remote, 3, jnp.where(selfish, 2, jnp.where(valid, 1, 0))).astype(jnp.int32)
    src = jnp.where(remote, owner * REQ_CAP + rank, jnp.where(valid, col_slot, 0))
    src = jnp.where(remote, jnp.clip(src, 0, peers * REQ_CAP - 1), jnp.clip(src, 0, BLK_DEV - 1)).astype(jnp.int32)
    tables = (src, junk_row, kind, asked)

    def exchange(out, rows_):
        got = lax.all_to_all(
            out.reshape(peers, REQ_CAP, rows_, genes), "cell", split_axis=0, concat_axis=0, tiled=True
        )
        return got.reshape(peers * REQ_CAP, rows_, genes)

    x0 = expression.reshape(BLK_DEV, BS, genes)
    inc0 = exchange(x0[asked], BS)
    cur_a, side_a = diffuse([a_sets[0]], [x0, inc0], deg_a, *tables, False, t_blk)
    inc_a = exchange(side_a, HALF)
    cur_b, side_b = diffuse([a_sets[1]], [x0, inc0], deg_b, *tables, False, t_blk)
    inc_b = exchange(side_b, HALF)
    cur, side = diffuse(a_sets, [cur_a, cur_b, inc_a, inc_b], deg_ab, *tables, False, t_blk)
    inc = exchange(side, BS)
    last, side = diffuse(a_sets, [cur, inc], deg_ab, *tables, True, t_blk)
    last = last.reshape(BLK_DEV * BS, genes)
    top_end = side[0]
    top_end = jnp.max(
        lax.all_to_all(jnp.broadcast_to(top_end[None, :], (peers, genes)), "cell", 0, 0, tiled=True), axis=0
    )
    return last * (top_start / top_end)[None, :]


def solution(mesh):
    return jax.shard_map(
        on_device,
        mesh=mesh,
        in_specs=(P("cell", "gene"), P("cell", "gene", None), P("cell"), P("cell"), P("cell")),
        out_specs=P("cell", "gene"),
        check_vma=False,
    )
```
